32 devices in a mesh: snd: 8 (over z, x), grp: 4 (over y, core).
Axes of the slice: x: 2, y: 2, z: 4, core: 2. Of those that a mesh axis runs over, the one named last changes fastest.
Arguments:
- sensitivity: bfloat16 [32, 16, 128, 128], P('snd', None, 'grp'), may hold values from -0.125 to 0.125
- gate_map: float32 [128, 40], P('grp'), may hold values from -0.5 to 0.5
- data_resid: float32 [32, 40], P('snd'), may hold values from -6 to 6
- data_weight: float32 [32, 40], P('snd'), may hold values from 0.3 to 3
- reg_weight: float32 [256, 128], P('snd'), may hold values from 0.3 to 3
- footprint: int32 [32, 16], P('snd'), may hold values from 0 to 255, as said below
- block_slot: int32 [256], replicated, may hold values from 0 to 255, as said below
Outputs:
- model_step: float32 [256, 128], P('snd')
- normal_residual: float32 [256, 128], P('snd')
The draws below stay inside these ranges and needn't reach their ends.
Inputs may be any that keep to these rules, and one draw needn't show every extreme that they name: Owner of block b is block_slot[b] // 32. In each aligned block of 4 soundings (the soundings of one index of snd), at most 16 of the 64 footprint entries lie on any one owner; the same owner receives exactly 16 from every such block. Entries may repeat. `block_slot`: A permutation: every storage row holds exactly one block.
All inputs are finite; a program needn't handle non-finite values.
Results may differ from the reference program's by a relative error of at most 0.0084.
Values may be sent and summed in bfloat16 or wider, within the bound.
No kernel may reach another device: no remote copies, remote signals or barrier semaphores. Data moves between devices by JAX's collectives and lax.ppermute only.
A program may use at most 64 MiB of HBM per device.

```python
import math
import jax
import jax.numpy as jnp
from jax import lax

S_DEV = 4
K = 16
CB = 128
FC = 128
NG = 40
ITERS = 2
SOUNDINGS = 32
B_DEV = 32
NB = 256
CAP = 16


def slot_table(key):
    return jax.random.permutation(jax.random.fold_in(key, 101), NB).astype(jnp.int32)


def draw_block_slot(key, part):
    return slot_table(key)


def draw_footprint(key, part):
    owners = SOUNDINGS // S_DEV
    entries = S_DEV * K
    block_of = jnp.argsort(slot_table(key)).astype(jnp.int32)
    busiest = jax.random.randint(jax.random.fold_in(key, 102), (), 0, owners).astype(jnp.int32)

    def one_device(device):
        device_key = jax.random.fold_in(jax.random.fold_in(key, 103), device)
        spread = CAP + jax.random.permutation(jax.random.fold_in(device_key, 1), owners * CAP - CAP)[:entries - CAP]
        picked = jnp.concatenate([jnp.arange(CAP, dtype=jnp.int32), spread.astype(jnp.int32)])
        owner_of = (picked // CAP + busiest) % owners
        local_row = jax.random.randint(jax.random.fold_in(device_key, 2), (entries,), 0, B_DEV).astype(jnp.int32)
        blocks = jnp.take(block_of, owner_of * B_DEV + local_row)
        shuffle = jax.random.permutation(jax.random.fold_in(device_key, 3), entries)
        return jnp.take(blocks, shuffle).reshape(S_DEV, K)
    drawn = jax.vmap(one_device)(jnp.arange(owners, dtype=jnp.int32))
    return drawn.reshape(SOUNDINGS, K).astype(jnp.int32)


def level_of(own_key, extent, pieces, least, largest):
    level, own = 1.0, jax.random.fold_in(own_key, 6)
    for axis_at, blocks in pieces:
        draws = jnp.exp(jax.random.uniform(jax.random.fold_in(own, axis_at), (blocks,), jnp.float32, least / len(pieces), largest / len(pieces)))
        level = level * jnp.repeat(draws, extent[axis_at] // blocks).reshape([-1 if axis == axis_at else 1 for axis in range(len(extent))])
    return level


def scatter_about(own_key, extent, scale, limit, shards=(), kind=jnp.bfloat16):
    values = scale * jax.random.normal(own_key, extent, jnp.float32)
    if shards:
        values = values * level_of(own_key, extent, shards, -0.22, 0.18)
    return jnp.clip(values, -limit, limit).astype(kind)


def setup_inputs(seed: int = 0) -> dict:
    seeds = jax.random.split(jax.random.key(seed), 8)
    sensitivity = scatter_about(seeds[0], (SOUNDINGS, K, FC, CB), (K * CB) ** -0.5, 0.125, ((0, 8), (2, 4)))
    gate_map = scatter_about(seeds[1], (FC, NG), FC ** -0.5, 0.5, ((0, 4),), jnp.float32)
    data_resid = scatter_about(seeds[2], (SOUNDINGS, NG), 1.0, 6.0, ((0, 8),), jnp.float32)
    data_weight = jnp.clip(jnp.exp(math.log(3.0) - 2.3025851 * jax.random.uniform(seeds[3], (SOUNDINGS, NG), jnp.float32) ** level_of(seeds[3], (SOUNDINGS, NG), ((0, 8),), -0.2, 0.2)), 0.3, 3.0)
    reg_weight = jnp.clip(jnp.exp(math.log(3.0) - 2.3025851 * jax.random.uniform(seeds[4], (NB, CB), jnp.float32) ** level_of(seeds[4], (NB, CB), ((0, 8),), -0.2, 0.2)), 0.3, 3.0)
    footprint = draw_footprint(jax.random.fold_in(seeds[7], 71), 0)
    block_slot = draw_block_slot(jax.random.fold_in(seeds[7], 71), 0)
    return {"sensitivity": sensitivity, "gate_map": gate_map, "data_resid": data_resid, "data_weight": data_weight, "reg_weight": reg_weight, "footprint": footprint, "block_slot": block_slot}


precise = lax.Precision.HIGHEST


def reference(sensitivity, gate_map, data_resid, data_weight, reg_weight, footprint, block_slot):
    slot_rows = jnp.take(block_slot, footprint, axis=0).astype(jnp.int32)
    sens_full = sensitivity.astype(jnp.float32)
    block_cells = reg_weight.shape[1]

    def forward(field):
        fetched = jnp.take(field, slot_rows, axis=0).astype(jnp.bfloat16)
        fetched = lax.optimization_barrier(fetched).astype(jnp.float32)
        response = jnp.einsum("skfc,skc->sf", sens_full, fetched, precision=precise)
        return jnp.dot(response, gate_map, precision=precise)

    def adjoint(weighted):
        back_freq = jnp.dot(weighted, gate_map.T, precision=precise).astype(jnp.bfloat16)
        back_freq = lax.optimization_barrier(back_freq).astype(jnp.float32)
        contribution = jnp.einsum("skfc,sf->skc", sens_full, back_freq, precision=precise)
        summed = jnp.zeros(reg_weight.shape, jnp.float32)
        return summed.at[slot_rows.reshape(-1)].add(contribution.reshape(-1, block_cells))

    right_side = adjoint(data_weight * data_resid)
    model_step = jnp.zeros(reg_weight.shape, jnp.float32)
    residual = right_side
    direction = right_side
    norm_now = jnp.sum(residual * residual)
    for iteration in range(ITERS):
        predicted = forward(direction)
        weighted = data_weight * predicted
        curvature = jnp.sum(predicted * weighted) + jnp.sum(reg_weight * direction * direction)
        image_cells = adjoint(weighted) + reg_weight * direction
        step_size = norm_now / curvature
        model_step = model_step + step_size * direction
        residual = residual - step_size * image_cells
        norm_next = jnp.sum(residual * residual)
        direction = residual + (norm_next / norm_now) * direction
        norm_now = norm_next
    return model_step, residual
```

```python
import jax
import jax.numpy as jnp
from jax import lax
from jax.sharding import PartitionSpec as P

ITERS = 2


precise = lax.Precision.HIGHEST


def body(sensitivity, gate_map, data_resid, data_weight, reg_weight, footprint, block_slot):
    owners = lax.axis_size("snd")
    members = lax.axis_size("grp")
    soundings, per_sounding = footprint.shape
    blocks_dev, block_cells = reg_weight.shape
    entries = soundings * per_sounding
    capacity = members * max(1, 2 * entries // (members * owners))
    slot_rows = jnp.take(block_slot, footprint.reshape(-1), axis=0)
    owner_of = slot_rows // blocks_dev
    local_of = slot_rows % blocks_dev
    onehot = (owner_of[:, None] == jnp.arange(owners, dtype=jnp.int32)[None, :]).astype(jnp.int32)
    before = jnp.cumsum(onehot, axis=0) - onehot
    rank_of = jnp.sum(before * onehot, axis=1)
    position = owner_of * capacity + rank_of
    request = jnp.full((owners * capacity,), -1, jnp.int32).at[position].set(local_of)

    def extra_row(values):
        values = jnp.broadcast_to(values.astype(jnp.float32), (owners, values.shape[-1]))
        row = jnp.zeros((owners, block_cells), jnp.float32).at[:, : values.shape[1]].set(values)
        return row[:, None, :]

    def contributions(weighted):
        back_freq = jnp.dot(
            weighted, gate_map.T, precision=precise, preferred_element_type=jnp.float32
        ).astype(jnp.bfloat16)
        contribution = jnp.einsum(
            "skfc,sf->skc", sensitivity, back_freq, preferred_element_type=jnp.float32
        )
        return contribution.reshape(entries, block_cells)

    def send_back(contribution, extra):
        outgoing = jnp.zeros((owners * capacity, block_cells), jnp.float32)
        outgoing = outgoing.at[position].set(contribution)
        outgoing = jnp.concatenate([outgoing.reshape(owners, capacity, block_cells), extra], axis=1)
        outgoing = jnp.broadcast_to(
            outgoing[:, None], (owners, members, capacity + 1, block_cells)
        ).reshape(owners * members, capacity + 1, block_cells)
        returned = lax.all_to_all(outgoing, ("snd", "grp"), 0, 0, tiled=True)
        returned = returned.reshape(owners, members, capacity + 1, block_cells)
        summed = jnp.sum(returned[:, :, :capacity, :], axis=1)
        return summed.reshape(owners * capacity, block_cells), returned[:, 0, capacity, :]

    right_partial, first_extra = send_back(
        contributions(data_weight * data_resid),
        extra_row(request.reshape(owners, capacity)),
    )
    incoming = first_extra[:, :capacity].astype(jnp.int32)
    live_slot = incoming >= 0
    safe_index = jnp.maximum(incoming, 0)
    owner_table = jnp.logical_and(
        safe_index.reshape(-1)[None, :] == jnp.arange(blocks_dev, dtype=jnp.int32)[:, None],
        live_slot.reshape(-1)[None, :],
    ).astype(jnp.float32)

    def gather_cells(summed):
        return jnp.dot(owner_table, summed, precision=precise, preferred_element_type=jnp.float32)

    right_side = gather_cells(right_partial)
    model_step = jnp.zeros(reg_weight.shape, jnp.float32)
    residual = right_side
    direction = right_side
    fetched_dir = None
    norm_now = None
    for iteration in range(ITERS):
        local_norm = jnp.sum(residual * residual)
        replies = jnp.where(
            live_slot[:, :, None],
            jnp.take(residual, safe_index, axis=0),
            jnp.zeros((), jnp.float32),
        )
        replies = jnp.concatenate([replies, extra_row(local_norm[None])], axis=1)
        arrived = lax.all_to_all(replies, "snd", 0, 0, tiled=True)
        norm_next = jnp.sum(arrived[:, capacity, 0])
        fetched_res = jnp.take(
            arrived[:, :capacity].reshape(owners * capacity, block_cells), position, axis=0
        )
        if iteration == 0:
            fetched_dir = fetched_res
        else:
            ratio = norm_next / norm_now
            direction = residual + ratio * direction
            fetched_dir = fetched_res + ratio * fetched_dir
        norm_now = norm_next
        forward_fetched = fetched_dir.astype(jnp.bfloat16).reshape(
            soundings, per_sounding, block_cells
        )
        response = jnp.einsum(
            "skfc,skc->sf", sensitivity, forward_fetched, preferred_element_type=jnp.float32
        )
        partial_gates = jnp.dot(
            response, gate_map, precision=precise, preferred_element_type=jnp.float32
        )
        predicted = lax.psum(partial_gates, "grp")
        weighted = data_weight * predicted
        local_curve = jnp.sum(predicted * weighted) + jnp.sum(reg_weight * direction * direction)
        image_partial, curve_extra = send_back(contributions(weighted), extra_row(local_curve[None]))
        curvature = jnp.sum(curve_extra[:, 0])
        image_cells = gather_cells(image_partial) + reg_weight * direction
        step_size = norm_now / curvature
        model_step = model_step + step_size * direction
        residual = residual - step_size * image_cells
    return (model_step, residual)


def solution(mesh):
    in_specs = (
        P("snd", None, "grp", None),
        P("grp", None),
        P("snd", None),
        P("snd", None),
        P("snd", None),
        P("snd", None),
        P(),
    )
    out_specs = (P("snd", None), P("snd", None))
    return jax.shard_map(body, mesh=mesh, in_specs=in_specs, out_specs=out_specs, check_vma=False)
```

```python
import jax
import jax.numpy as jnp
from jax import lax
from jax.sharding import PartitionSpec as P

ITERS = 2


precise = lax.Precision.HIGHEST


def body(sensitivity, gate_map, data_resid, data_weight, reg_weight, footprint, block_slot):
    owners = lax.axis_size("snd")
    members = lax.axis_size("grp")
    soundings, per_sounding = footprint.shape
    blocks_dev, block_cells = reg_weight.shape
    entries = soundings * per_sounding
    capacity = members * max(1, 2 * entries // (members * owners))
    slot_rows = jnp.take(block_slot, footprint.reshape(-1), axis=0)
    owner_of = slot_rows // blocks_dev
    local_of = slot_rows % blocks_dev
    onehot = (owner_of[:, None] == jnp.arange(owners, dtype=jnp.int32)[None, :]).astype(jnp.int32)
    before = jnp.cumsum(onehot, axis=0) - onehot
    rank_of = jnp.sum(before * onehot, axis=1)
    position = owner_of * capacity + rank_of
    request = jnp.full((owners * capacity,), -1, jnp.int32).at[position].set(local_of)

    def extra_row(value):
        return jnp.broadcast_to(value.astype(jnp.float32), (owners, 1, block_cells))

    def contributions(weighted):
        back_freq = jnp.dot(
            weighted, gate_map.T, precision=precise, preferred_element_type=jnp.float32
        ).astype(jnp.bfloat16)
        contribution = jnp.einsum(
            "skfc,sf->skc", sensitivity, back_freq, preferred_element_type=jnp.float32
        )
        return contribution.reshape(entries, block_cells)

    def send_back(contribution, extra):
        outgoing = jnp.zeros((owners * capacity, block_cells), jnp.float32)
        outgoing = outgoing.at[position].set(contribution)
        outgoing = jnp.concatenate([outgoing.reshape(owners, capacity, block_cells), extra], axis=1)
        outgoing = jnp.broadcast_to(
            outgoing[:, None], (owners, members, capacity + 1, block_cells)
        ).reshape(owners * members, capacity + 1, block_cells)
        returned = lax.all_to_all(outgoing, ("snd", "grp"), 0, 0, tiled=True)
        returned = returned.reshape(owners, members, capacity + 1, block_cells)
        summed = jnp.sum(returned[:, :, :capacity, :], axis=1)
        return summed.reshape(owners * capacity, block_cells), returned[:, 0, capacity, :]

    right_partial, first_extra = send_back(
        contributions(data_weight * data_resid),
        jnp.pad(
            request.reshape(owners, 1, capacity).astype(jnp.float32),
            ((0, 0), (0, 0), (0, block_cells - capacity)),
        ),
    )
    incoming = first_extra[:, :capacity].astype(jnp.int32)
    live_slot = incoming >= 0
    safe_index = jnp.maximum(incoming, 0)
    owner_table = jnp.logical_and(
        safe_index.reshape(-1)[None, :] == jnp.arange(blocks_dev, dtype=jnp.int32)[:, None],
        live_slot.reshape(-1)[None, :],
    ).astype(jnp.float32)

    def gather_cells(summed):
        return jnp.dot(owner_table, summed, precision=precise, preferred_element_type=jnp.float32)

    right_side = gather_cells(right_partial)
    model_step = jnp.zeros(reg_weight.shape, jnp.float32)
    residual = right_side
    direction = right_side
    fetched_dir = None
    norm_now = None
    for iteration in range(ITERS):
        local_norm = jnp.sum(residual * residual)
        replies = jnp.where(
            live_slot[:, :, None],
            jnp.take(residual, safe_index, axis=0),
            jnp.zeros((), jnp.float32),
        )
        replies = jnp.concatenate([replies, extra_row(local_norm)], axis=1)
        arrived = lax.all_to_all(replies, "snd", 0, 0, tiled=True)
        norm_next = jnp.sum(arrived[:, capacity, :], axis=0)
        fetched_res = jnp.take(
            arrived[:, :capacity].reshape(owners * capacity, block_cells), position, axis=0
        )
        if iteration == 0:
            fetched_dir = fetched_res
        else:
            ratio = norm_next / norm_now
            direction = residual + ratio * direction
            fetched_dir = fetched_res + ratio * fetched_dir
        norm_now = norm_next
        forward_fetched = fetched_dir.astype(jnp.bfloat16).reshape(
            soundings, per_sounding, block_cells
        )
        response = jnp.einsum(
            "skfc,skc->sf", sensitivity, forward_fetched, preferred_element_type=jnp.float32
        )
        partial_gates = jnp.dot(
            response, gate_map, precision=precise, preferred_element_type=jnp.float32
        )
        predicted = lax.psum(partial_gates, "grp")
        weighted = data_weight * predicted
        local_curve = jnp.sum(predicted * weighted) + jnp.sum(reg_weight * direction * direction)
        image_partial, curve_extra = send_back(contributions(weighted), extra_row(local_curve))
        curvature = jnp.sum(curve_extra, axis=0)
        image_cells = gather_cells(image_partial) + reg_weight * direction
        step_size = norm_now / curvature
        model_step = model_step + step_size * direction
        residual = residual - step_size * image_cells
    return (model_step, residual)


def solution(mesh):
    in_specs = (
        P("snd", None, "grp", None),
        P("grp", None),
        P("snd", None),
        P("snd", None),
        P("snd", None),
        P("snd", None),
        P(),
    )
    out_specs = (P("snd", None), P("snd", None))
    return jax.shard_map(body, mesh=mesh, in_specs=in_specs, out_specs=out_specs, check_vma=False)
```

```python
import jax
import jax.numpy as jnp
from jax import lax
from jax.sharding import PartitionSpec as P

ITERS = 2


precise = lax.Precision.HIGHEST


def body(sensitivity, gate_map, data_resid, data_weight, reg_weight, footprint, block_slot):
    owners = lax.axis_size("snd")
    members = lax.axis_size("grp")
    soundings, per_sounding = footprint.shape
    blocks_dev, block_cells = reg_weight.shape
    entries = soundings * per_sounding
    capacity = members * max(1, 2 * entries // (members * owners))
    slot_rows = jnp.take(block_slot, footprint.reshape(-1), axis=0)
    owner_of = slot_rows // blocks_dev
    local_of = slot_rows % blocks_dev
    onehot = (owner_of[:, None] == jnp.arange(owners, dtype=jnp.int32)[None, :]).astype(jnp.int32)
    before = jnp.cumsum(onehot, axis=0) - onehot
    rank_of = jnp.sum(before * onehot, axis=1)
    position = owner_of * capacity + rank_of
    request = jnp.full((owners * capacity,), -1, jnp.int32).at[position].set(local_of)

    def extra_row(value):
        return jnp.broadcast_to(value.astype(jnp.float32), (owners, 1, block_cells))

    slots = owners * capacity
    slot_entry = jnp.full((slots,), -1, jnp.int32).at[position].set(
        jnp.arange(entries, dtype=jnp.int32)
    )
    slot_live = slot_entry >= 0
    slot_source = jnp.maximum(slot_entry, 0)
    slot_sounding = slot_source // per_sounding
    sens_slots = jnp.where(
        slot_live[:, None, None],
        jnp.take(sensitivity.reshape(entries, -1, block_cells), slot_source, axis=0),
        jnp.zeros((), sensitivity.dtype),
    )
    sounding_table = jnp.logical_and(
        slot_sounding[None, :] == jnp.arange(soundings, dtype=jnp.int32)[:, None],
        slot_live[None, :],
    ).astype(jnp.bfloat16)

    def contributions(weighted):
        back_freq = jnp.dot(
            weighted, gate_map.T, precision=precise, preferred_element_type=jnp.float32
        ).astype(jnp.bfloat16)
        back_slots = jnp.dot(
            sounding_table.T, back_freq, preferred_element_type=jnp.float32
        ).astype(jnp.bfloat16)
        return jnp.einsum("pfc,pf->pc", sens_slots, back_slots, preferred_element_type=jnp.float32)

    def send_back(outgoing, extra):
        outgoing = jnp.concatenate([outgoing.reshape(owners, capacity, block_cells), extra], axis=1)
        outgoing = jnp.broadcast_to(
            outgoing[:, None], (owners, members, capacity + 1, block_cells)
        ).reshape(owners * members, capacity + 1, block_cells)
        returned = lax.all_to_all(outgoing, ("snd", "grp"), 0, 0, tiled=True)
        returned = returned.reshape(owners, members, capacity + 1, block_cells)
        summed = jnp.sum(returned[:, :, :capacity, :], axis=1)
        return summed.reshape(slots, block_cells), returned[:, 0, capacity, :]

    right_partial, first_extra = send_back(
        contributions(data_weight * data_resid),
        jnp.pad(
            request.reshape(owners, 1, capacity).astype(jnp.float32),
            ((0, 0), (0, 0), (0, block_cells - capacity)),
        ),
    )
    incoming = first_extra[:, :capacity].astype(jnp.int32)
    live_slot = incoming >= 0
    safe_index = jnp.maximum(incoming, 0)
    owner_table = jnp.logical_and(
        safe_index.reshape(-1)[None, :] == jnp.arange(blocks_dev, dtype=jnp.int32)[:, None],
        live_slot.reshape(-1)[None, :],
    ).astype(jnp.float32)

    def gather_cells(summed):
        return jnp.dot(owner_table, summed, precision=precise, preferred_element_type=jnp.float32)

    right_side = gather_cells(right_partial)
    model_step = jnp.zeros(reg_weight.shape, jnp.float32)
    residual = right_side
    direction = right_side
    fetched_dir = None
    norm_now = None
    for iteration in range(ITERS):
        local_norm = jnp.sum(residual * residual)
        replies = jnp.where(
            live_slot[:, :, None],
            jnp.take(residual, safe_index, axis=0),
            jnp.zeros((), jnp.float32),
        )
        replies = jnp.concatenate([replies, extra_row(local_norm)], axis=1)
        arrived = lax.all_to_all(replies, "snd", 0, 0, tiled=True)
        norm_next = jnp.sum(arrived[:, capacity, :], axis=0)
        fetched_res = arrived[:, :capacity].reshape(slots, block_cells)
        if iteration == 0:
            fetched_dir = fetched_res
        else:
            ratio = norm_next / norm_now
            direction = residual + ratio * direction
            fetched_dir = fetched_res + ratio * fetched_dir
        norm_now = norm_next
        forward_fetched = sounding_table[:, :, None] * fetched_dir.astype(jnp.bfloat16)[None]
        response = jnp.einsum(
            "spc,pfc->sf", forward_fetched, sens_slots, preferred_element_type=jnp.float32
        )
        partial_gates = jnp.dot(
            response, gate_map, precision=precise, preferred_element_type=jnp.float32
        )
        predicted = lax.psum(partial_gates, "grp")
        weighted = data_weight * predicted
        local_curve = jnp.sum(predicted * weighted) + jnp.sum(reg_weight * direction * direction)
        image_partial, curve_extra = send_back(contributions(weighted), extra_row(local_curve))
        curvature = jnp.sum(curve_extra, axis=0)
        image_cells = gather_cells(image_partial) + reg_weight * direction
        step_size = norm_now / curvature
        model_step = model_step + step_size * direction
        residual = residual - step_size * image_cells
    return (model_step, residual)


def solution(mesh):
    in_specs = (
        P("snd", None, "grp", None),
        P("grp", None),
        P("snd", None),
        P("snd", None),
        P("snd", None),
        P("snd", None),
        P(),
    )
    out_specs = (P("snd", None), P("snd", None))
    return jax.shard_map(body, mesh=mesh, in_specs=in_specs, out_specs=out_specs, check_vma=False)
```

```python
import jax
import jax.numpy as jnp
from jax import lax
from jax.sharding import PartitionSpec as P

ITERS = 2


precise = lax.Precision.HIGHEST


def body(sensitivity, gate_map, data_resid, data_weight, reg_weight, footprint, block_slot):
    owners = lax.axis_size("snd")
    members = lax.axis_size("grp")
    soundings, per_sounding = footprint.shape
    blocks_dev, block_cells = reg_weight.shape
    entries = soundings * per_sounding
    capacity = members * max(1, 2 * entries // (members * owners))
    slot_rows = jnp.take(block_slot, footprint.reshape(-1), axis=0)
    owner_of = slot_rows // blocks_dev
    local_of = slot_rows % blocks_dev
    onehot = (owner_of[:, None] == jnp.arange(owners, dtype=jnp.int32)[None, :]).astype(jnp.int32)
    before = jnp.cumsum(onehot, axis=0) - onehot
    rank_of = jnp.sum(before * onehot, axis=1)
    position = owner_of * capacity + rank_of
    slots = owners * capacity
    slot_hit = position[None, :] == jnp.arange(slots, dtype=jnp.int32)[:, None]
    slot_live = jnp.any(slot_hit, axis=1)
    request = jnp.where(slot_live, jnp.sum(jnp.where(slot_hit, local_of[None, :], 0), axis=1), -1)

    def extra_row(value):
        return jnp.broadcast_to(value.astype(jnp.float32), (owners, 1, block_cells))

    slot_table = slot_hit.astype(sensitivity.dtype)
    sens_slots = jnp.dot(
        slot_table, sensitivity.reshape(entries, -1), preferred_element_type=jnp.float32
    ).astype(sensitivity.dtype).reshape(slots, -1, block_cells)
    entry_sounding = jnp.arange(entries, dtype=jnp.int32) // per_sounding
    slot_sounding = jnp.sum(jnp.where(slot_hit, entry_sounding[None, :], 0), axis=1)
    sounding_table = jnp.logical_and(
        slot_sounding[None, :] == jnp.arange(soundings, dtype=jnp.int32)[:, None],
        slot_live[None, :],
    ).astype(jnp.bfloat16)

    def contributions(weighted):
        back_freq = jnp.dot(
            weighted, gate_map.T, precision=precise, preferred_element_type=jnp.float32
        ).astype(jnp.bfloat16)
        back_slots = jnp.dot(
            sounding_table.T, back_freq, preferred_element_type=jnp.float32
        ).astype(jnp.bfloat16)
        return jnp.einsum("pfc,pf->pc", sens_slots, back_slots, preferred_element_type=jnp.float32)

    def send_back(outgoing, extra):
        outgoing = jnp.concatenate([outgoing.reshape(owners, capacity, block_cells), extra], axis=1)
        row_len = (capacity + 1) * block_cells
        outgoing = jnp.broadcast_to(
            outgoing.reshape(owners, 1, 1, row_len), (owners, members, 1, row_len)
        ).reshape(owners * members, 1, row_len)
        returned = lax.all_to_all(outgoing, ("snd", "grp"), 0, 0, tiled=True)
        returned = returned.reshape(owners, members, capacity + 1, block_cells)
        summed = jnp.sum(returned[:, :, :capacity, :], axis=1)
        return summed.reshape(slots, block_cells), returned[:, 0, capacity, :]

    right_partial, first_extra = send_back(
        contributions(data_weight * data_resid),
        jnp.pad(
            request.reshape(owners, 1, capacity).astype(jnp.float32),
            ((0, 0), (0, 0), (0, block_cells - capacity)),
        ),
    )
    incoming = first_extra[:, :capacity].astype(jnp.int32)
    live_slot = incoming >= 0
    safe_index = jnp.maximum(incoming, 0)
    owner_table = jnp.logical_and(
        safe_index.reshape(-1)[None, :] == jnp.arange(blocks_dev, dtype=jnp.int32)[:, None],
        live_slot.reshape(-1)[None, :],
    ).astype(jnp.float32)

    def gather_cells(summed):
        return jnp.dot(owner_table, summed, precision=precise, preferred_element_type=jnp.float32)

    right_side = gather_cells(right_partial)
    model_step = jnp.zeros(reg_weight.shape, jnp.float32)
    residual = right_side
    direction = right_side
    fetched_dir = None
    norm_now = None
    for iteration in range(ITERS):
        local_norm = jnp.sum(residual * residual)
        replies = jnp.where(
            live_slot[:, :, None],
            jnp.take(residual, safe_index, axis=0),
            jnp.zeros((), jnp.float32),
        )
        replies = jnp.concatenate([replies, extra_row(local_norm)], axis=1)
        arrived = lax.all_to_all(replies, "snd", 0, 0, tiled=True)
        norm_next = jnp.sum(arrived[:, capacity, :], axis=0)
        fetched_res = arrived[:, :capacity].reshape(slots, block_cells)
        if iteration == 0:
            fetched_dir = fetched_res
        else:
            ratio = norm_next / norm_now
            direction = residual + ratio * direction
            fetched_dir = fetched_res + ratio * fetched_dir
        norm_now = norm_next
        forward_fetched = sounding_table[:, :, None] * fetched_dir.astype(jnp.bfloat16)[None]
        response = jnp.einsum(
            "spc,pfc->sf", forward_fetched, sens_slots, preferred_element_type=jnp.float32
        )
        partial_gates = jnp.dot(
            response, gate_map, precision=precise, preferred_element_type=jnp.float32
        )
        predicted = lax.psum(partial_gates, "grp")
        weighted = data_weight * predicted
        local_curve = jnp.sum(predicted * weighted) + jnp.sum(reg_weight * direction * direction)
        image_partial, curve_extra = send_back(contributions(weighted), extra_row(local_curve))
        curvature = jnp.sum(curve_extra, axis=0)
        image_cells = gather_cells(image_partial) + reg_weight * direction
        step_size = norm_now / curvature
        model_step = model_step + step_size * direction
        residual = residual - step_size * image_cells
    return (model_step, residual)


def solution(mesh):
    in_specs = (
        P("snd", None, "grp", None),
        P("grp", None),
        P("snd", None),
        P("snd", None),
        P("snd", None),
        P("snd", None),
        P(),
    )
    out_specs = (P("snd", None), P("snd", None))
    return jax.shard_map(body, mesh=mesh, in_specs=in_specs, out_specs=out_specs, check_vma=False)
```

```python
import jax
import jax.numpy as jnp
from jax import lax
from jax.sharding import PartitionSpec as P

ITERS = 2


precise = lax.Precision.HIGHEST


def body(sensitivity, gate_map, data_resid, data_weight, reg_weight, footprint, block_slot):
    owners = lax.axis_size("snd")
    members = lax.axis_size("grp")
    soundings, per_sounding = footprint.shape
    blocks_dev, block_cells = reg_weight.shape
    entries = soundings * per_sounding
    capacity = members * max(1, 2 * entries // (members * owners))
    blocks = block_slot.shape[0]
    slot_rows = jnp.sum(
        jnp.where(
            footprint[:, :, None] == jnp.arange(blocks, dtype=jnp.int32)[None, None, :],
            block_slot[None, None, :],
            0,
        ),
        axis=2,
    )
    owner_of = slot_rows // blocks_dev
    local_of = slot_rows % blocks_dev
    entry_id = (
        jnp.arange(soundings, dtype=jnp.int32)[:, None] * per_sounding
        + jnp.arange(per_sounding, dtype=jnp.int32)[None, :]
    )
    earlier_same = jnp.logical_and(
        owner_of[:, :, None, None] == owner_of[None, None, :, :],
        entry_id[None, None, :, :] < entry_id[:, :, None, None],
    )
    rank_of = jnp.sum(earlier_same.astype(jnp.int32), axis=(2, 3))
    slots = owners * capacity
    slot_hit = jnp.logical_and(
        owner_of[None, None] == jnp.arange(owners, dtype=jnp.int32)[:, None, None, None],
        rank_of[None, None] == jnp.arange(capacity, dtype=jnp.int32)[None, :, None, None],
    )
    slot_live = jnp.any(slot_hit, axis=(2, 3))
    request = jnp.where(
        slot_live, jnp.sum(jnp.where(slot_hit, local_of[None, None], 0), axis=(2, 3)), -1
    )

    def extra_row(value):
        return jnp.broadcast_to(value.astype(jnp.float32), (owners, 1, block_cells))

    sens_slots = jnp.einsum(
        "oqsk,skfc->oqfc",
        slot_hit.astype(sensitivity.dtype),
        sensitivity,
        preferred_element_type=jnp.float32,
    ).astype(sensitivity.dtype).reshape(slots, -1, block_cells)
    slot_sounding = jnp.sum(
        jnp.where(slot_hit, jnp.arange(soundings, dtype=jnp.int32)[:, None], 0), axis=(2, 3)
    ).reshape(slots)
    slot_live = slot_live.reshape(slots)
    sounding_table = jnp.logical_and(
        slot_sounding[None, :] == jnp.arange(soundings, dtype=jnp.int32)[:, None],
        slot_live[None, :],
    ).astype(jnp.bfloat16)

    def contributions(weighted):
        back_freq = jnp.dot(
            weighted, gate_map.T, precision=precise, preferred_element_type=jnp.float32
        ).astype(jnp.bfloat16)
        back_slots = jnp.dot(
            sounding_table.T, back_freq, preferred_element_type=jnp.float32
        ).astype(jnp.bfloat16)
        return jnp.einsum("pfc,pf->pc", sens_slots, back_slots, preferred_element_type=jnp.float32)

    def send_back(outgoing, extra):
        outgoing = jnp.concatenate([outgoing.reshape(owners, capacity, block_cells), extra], axis=1)
        row_len = (capacity + 1) * block_cells
        outgoing = jnp.broadcast_to(
            outgoing.reshape(owners, 1, 1, row_len), (owners, members, 1, row_len)
        ).reshape(owners * members, 1, row_len)
        returned = lax.all_to_all(outgoing, ("snd", "grp"), 0, 0, tiled=True)
        returned = returned.reshape(owners, members, capacity + 1, block_cells)
        summed = jnp.sum(returned[:, :, :capacity, :], axis=1)
        return summed.reshape(slots, block_cells), returned[:, 0, capacity, :]

    right_partial, first_extra = send_back(
        contributions(data_weight * data_resid),
        jnp.pad(
            request[:, None, :].astype(jnp.float32),
            ((0, 0), (0, 0), (0, block_cells - capacity)),
        ),
    )
    incoming = first_extra[:, :capacity].astype(jnp.int32)
    live_slot = incoming >= 0
    safe_index = jnp.maximum(incoming, 0)
    owner_table = jnp.logical_and(
        safe_index.reshape(-1)[None, :] == jnp.arange(blocks_dev, dtype=jnp.int32)[:, None],
        live_slot.reshape(-1)[None, :],
    ).astype(jnp.float32)

    def gather_cells(summed):
        return jnp.dot(owner_table, summed, precision=precise, preferred_element_type=jnp.float32)

    right_side = gather_cells(right_partial)
    model_step = jnp.zeros(reg_weight.shape, jnp.float32)
    residual = right_side
    direction = right_side
    fetched_dir = None
    norm_now = None
    for iteration in range(ITERS):
        local_norm = jnp.sum(residual * residual)
        replies = jnp.where(
            live_slot[:, :, None],
            jnp.take(residual, safe_index, axis=0),
            jnp.zeros((), jnp.float32),
        )
        replies = jnp.concatenate([replies, extra_row(local_norm)], axis=1)
        arrived = lax.all_to_all(replies, "snd", 0, 0, tiled=True)
        norm_next = jnp.sum(arrived[:, capacity, :], axis=0)
        fetched_res = arrived[:, :capacity].reshape(slots, block_cells)
        if iteration == 0:
            fetched_dir = fetched_res
        else:
            ratio = norm_next / norm_now
            direction = residual + ratio * direction
            fetched_dir = fetched_res + ratio * fetched_dir
        norm_now = norm_next
        forward_fetched = sounding_table[:, :, None] * fetched_dir.astype(jnp.bfloat16)[None]
        response = jnp.einsum(
            "spc,pfc->sf", forward_fetched, sens_slots, preferred_element_type=jnp.float32
        )
        partial_gates = jnp.dot(
            response, gate_map, precision=precise, preferred_element_type=jnp.float32
        )
        predicted = lax.psum(partial_gates, "grp")
        weighted = data_weight * predicted
        local_curve = jnp.sum(predicted * weighted) + jnp.sum(reg_weight * direction * direction)
        image_partial, curve_extra = send_back(contributions(weighted), extra_row(local_curve))
        curvature = jnp.sum(curve_extra, axis=0)
        image_cells = gather_cells(image_partial) + reg_weight * direction
        step_size = norm_now / curvature
        model_step = model_step + step_size * direction
        residual = residual - step_size * image_cells
    return (model_step, residual)


def solution(mesh):
    in_specs = (
        P("snd", None, "grp", None),
        P("grp", None),
        P("snd", None),
        P("snd", None),
        P("snd", None),
        P("snd", None),
        P(),
    )
    out_specs = (P("snd", None), P("snd", None))
    return jax.shard_map(body, mesh=mesh, in_specs=in_specs, out_specs=out_specs, check_vma=False)
```

```python
import jax
import jax.numpy as jnp
from jax import lax
from jax.sharding import PartitionSpec as P

ITERS = 2


precise = lax.Precision.HIGHEST


def body(sensitivity, gate_map, data_resid, data_weight, reg_weight, footprint, block_slot):
    owners = lax.axis_size("snd")
    members = lax.axis_size("grp")
    soundings, per_sounding = footprint.shape
    blocks_dev, block_cells = reg_weight.shape
    entries = soundings * per_sounding
    capacity = members * max(1, 2 * entries // (members * owners))
    blocks = block_slot.shape[0]
    slot_rows = jnp.sum(
        jnp.where(
            footprint[:, :, None] == jnp.arange(blocks, dtype=jnp.int32)[None, None, :],
            block_slot[None, None, :],
            0,
        ),
        axis=2,
    )
    owner_of = slot_rows // blocks_dev
    local_of = slot_rows % blocks_dev
    entry_id = (
        jnp.arange(soundings, dtype=jnp.int32)[:, None] * per_sounding
        + jnp.arange(per_sounding, dtype=jnp.int32)[None, :]
    )
    earlier_same = jnp.logical_and(
        owner_of[:, :, None, None] == owner_of[None, None, :, :],
        entry_id[None, None, :, :] < entry_id[:, :, None, None],
    )
    rank_of = jnp.sum(earlier_same.astype(jnp.int32), axis=(2, 3))
    slots = owners * capacity
    slot_hit = jnp.logical_and(
        owner_of[None, None] == jnp.arange(owners, dtype=jnp.int32)[:, None, None, None],
        rank_of[None, None] == jnp.arange(capacity, dtype=jnp.int32)[None, :, None, None],
    )
    slot_live = jnp.any(slot_hit, axis=(2, 3))
    request = jnp.where(
        slot_live, jnp.sum(jnp.where(slot_hit, local_of[None, None], 0), axis=(2, 3)), -1
    )

    def extra_row(value):
        return jnp.broadcast_to(value.astype(jnp.float32), (owners, 1, block_cells))

    sens_slots = jnp.einsum(
        "oqsk,skfc->oqfc",
        slot_hit.astype(sensitivity.dtype),
        sensitivity,
        preferred_element_type=jnp.float32,
    ).astype(sensitivity.dtype).reshape(slots, -1, block_cells)
    slot_sounding = jnp.sum(
        jnp.where(slot_hit, jnp.arange(soundings, dtype=jnp.int32)[:, None], 0), axis=(2, 3)
    ).reshape(slots)
    slot_live = slot_live.reshape(slots)
    sounding_table = jnp.logical_and(
        slot_sounding[None, :] == jnp.arange(soundings, dtype=jnp.int32)[:, None],
        slot_live[None, :],
    ).astype(jnp.bfloat16)

    def contributions(weighted):
        back_freq = jnp.dot(
            weighted, gate_map.T, precision=precise, preferred_element_type=jnp.float32
        ).astype(jnp.bfloat16)
        back_slots = jnp.dot(
            sounding_table.T, back_freq, preferred_element_type=jnp.float32
        ).astype(jnp.bfloat16)
        return jnp.einsum("pfc,pf->pc", sens_slots, back_slots, preferred_element_type=jnp.float32)

    def send_back(outgoing, extra):
        outgoing = jnp.concatenate([outgoing.reshape(owners, capacity, block_cells), extra], axis=1)
        row_len = (capacity + 1) * block_cells
        outgoing = jnp.broadcast_to(
            outgoing.reshape(1, owners, row_len), (members, owners, row_len)
        ).reshape(members * owners, row_len)
        returned = lax.all_to_all(outgoing, ("grp", "snd"), 0, 0, tiled=True)
        returned = returned.reshape(members, owners, capacity + 1, block_cells)
        return returned[:, :, :capacity, :], returned[0, :, capacity, :]

    def split3(x):
        hi = lax.reduce_precision(x, exponent_bits=8, mantissa_bits=7)
        rest = x - hi
        mid = lax.reduce_precision(rest, exponent_bits=8, mantissa_bits=7)
        return jnp.stack([hi, mid, rest - mid]).astype(jnp.bfloat16)

    right_partial, first_extra = send_back(
        contributions(data_weight * data_resid),
        jnp.pad(
            request[:, None, :].astype(jnp.float32),
            ((0, 0), (0, 0), (0, block_cells - capacity)),
        ),
    )
    incoming = first_extra[:, :capacity].astype(jnp.int32)
    live_slot = incoming >= 0
    safe_index = jnp.maximum(incoming, 0)
    owner_table = jnp.logical_and(
        safe_index[None] == jnp.arange(blocks_dev, dtype=jnp.int32)[:, None, None],
        live_slot[None],
    )
    owner_table = jnp.broadcast_to(
        owner_table[:, None], (blocks_dev, members, owners, capacity)
    ).astype(jnp.bfloat16)
    reply_table = jnp.logical_and(
        safe_index[:, :, None] == jnp.arange(blocks_dev, dtype=jnp.int32)[None, None, :],
        live_slot[:, :, None],
    ).astype(jnp.bfloat16)

    def gather_cells(rows):
        parts = jnp.einsum(
            "rjoq,sjoqc->src", owner_table, split3(rows), preferred_element_type=jnp.float32
        )
        return (parts[0] + parts[1]) + parts[2]

    def pick_rows(field):
        parts = jnp.einsum(
            "oqr,src->soqc", reply_table, split3(field), preferred_element_type=jnp.float32
        )
        return (parts[0] + parts[1]) + parts[2]

    right_side = gather_cells(right_partial)
    model_step = jnp.zeros(reg_weight.shape, jnp.float32)
    residual = right_side
    direction = right_side
    fetched_dir = None
    norm_now = None
    for iteration in range(ITERS):
        local_norm = jnp.sum(residual * residual)
        replies = pick_rows(residual)
        replies = jnp.concatenate([replies, extra_row(local_norm)], axis=1)
        arrived = lax.all_to_all(replies, "snd", 0, 0, tiled=True)
        norm_next = jnp.sum(arrived[:, capacity, :], axis=0)
        fetched_res = arrived[:, :capacity].reshape(slots, block_cells)
        if iteration == 0:
            fetched_dir = fetched_res
        else:
            ratio = norm_next / norm_now
            direction = residual + ratio * direction
            fetched_dir = fetched_res + ratio * fetched_dir
        norm_now = norm_next
        forward_fetched = sounding_table[:, :, None] * fetched_dir.astype(jnp.bfloat16)[None]
        response = jnp.einsum(
            "spc,pfc->sf", forward_fetched, sens_slots, preferred_element_type=jnp.float32
        )
        partial_gates = jnp.dot(
            response, gate_map, precision=precise, preferred_element_type=jnp.float32
        )
        predicted = lax.psum(partial_gates, "grp")
        weighted = data_weight * predicted
        local_curve = jnp.sum(predicted * weighted) + jnp.sum(reg_weight * direction * direction)
        image_partial, curve_extra = send_back(contributions(weighted), extra_row(local_curve))
        curvature = jnp.sum(curve_extra, axis=0)
        image_cells = gather_cells(image_partial) + reg_weight * direction
        step_size = norm_now / curvature
        model_step = model_step + step_size * direction
        residual = residual - step_size * image_cells
    return (model_step, residual)


def solution(mesh):
    in_specs = (
        P("snd", None, "grp", None),
        P("grp", None),
        P("snd", None),
        P("snd", None),
        P("snd", None),
        P("snd", None),
        P(),
    )
    out_specs = (P("snd", None), P("snd", None))
    return jax.shard_map(body, mesh=mesh, in_specs=in_specs, out_specs=out_specs, check_vma=False)
```

```python
import jax
import jax.numpy as jnp
from jax import lax
from jax.sharding import PartitionSpec as P

ITERS = 2


precise = lax.Precision.HIGHEST


def body(sensitivity, gate_map, data_resid, data_weight, reg_weight, footprint, block_slot):
    owners = lax.axis_size("snd")
    members = lax.axis_size("grp")
    soundings, per_sounding = footprint.shape
    blocks_dev, block_cells = reg_weight.shape
    entries = soundings * per_sounding
    capacity = members * max(1, 2 * entries // (members * owners))
    blocks = block_slot.shape[0]
    slot_rows = jnp.sum(
        jnp.where(
            footprint[:, :, None] == jnp.arange(blocks, dtype=jnp.int32)[None, None, :],
            block_slot[None, None, :],
            0,
        ),
        axis=2,
    )
    owner_of = slot_rows // blocks_dev
    local_of = slot_rows % blocks_dev
    entry_id = (
        jnp.arange(soundings, dtype=jnp.int32)[:, None] * per_sounding
        + jnp.arange(per_sounding, dtype=jnp.int32)[None, :]
    )
    earlier_same = jnp.logical_and(
        owner_of[:, :, None, None] == owner_of[None, None, :, :],
        entry_id[None, None, :, :] < entry_id[:, :, None, None],
    )
    rank_of = jnp.sum(earlier_same.astype(jnp.int32), axis=(2, 3))
    slots = owners * capacity
    slot_hit = jnp.logical_and(
        owner_of[None, None] == jnp.arange(owners, dtype=jnp.int32)[:, None, None, None],
        rank_of[None, None] == jnp.arange(capacity, dtype=jnp.int32)[None, :, None, None],
    )
    slot_live = jnp.any(slot_hit, axis=(2, 3))
    request = jnp.where(
        slot_live, jnp.sum(jnp.where(slot_hit, local_of[None, None], 0), axis=(2, 3)), -1
    )

    def extra_row(value):
        return jnp.broadcast_to(value.astype(jnp.float32), (owners, 1, block_cells))

    sens_slots = jnp.einsum(
        "oqsk,skfc->foqc",
        slot_hit.astype(sensitivity.dtype),
        sensitivity,
        preferred_element_type=jnp.float32,
    ).astype(sensitivity.dtype).reshape(-1, slots, block_cells)
    slot_sounding = jnp.sum(
        jnp.where(slot_hit, jnp.arange(soundings, dtype=jnp.int32)[:, None], 0), axis=(2, 3)
    ).reshape(slots)
    slot_live = slot_live.reshape(slots)
    sounding_table = jnp.logical_and(
        slot_sounding[None, :] == jnp.arange(soundings, dtype=jnp.int32)[:, None],
        slot_live[None, :],
    ).astype(jnp.bfloat16)

    def contributions(weighted):
        back_freq = jnp.dot(
            weighted, gate_map.T, precision=precise, preferred_element_type=jnp.float32
        ).astype(jnp.bfloat16)
        back_slots = jnp.dot(
            back_freq.T, sounding_table, preferred_element_type=jnp.float32
        ).astype(jnp.bfloat16)
        return jnp.sum(
            sens_slots.astype(jnp.float32) * back_slots.astype(jnp.float32)[:, :, None], axis=0
        )

    def send_back(outgoing, extra):
        outgoing = jnp.concatenate([outgoing.reshape(owners, capacity, block_cells), extra], axis=1)
        row_len = (capacity + 1) * block_cells
        outgoing = jnp.broadcast_to(
            outgoing.reshape(1, owners, row_len), (members, owners, row_len)
        ).reshape(members * owners, row_len)
        returned = lax.all_to_all(outgoing, ("grp", "snd"), 0, 0, tiled=True)
        returned = returned.reshape(members, owners, capacity + 1, block_cells)
        return returned[:, :, :capacity, :], returned[0, :, capacity, :]

    def split3(x):
        hi = lax.reduce_precision(x, exponent_bits=8, mantissa_bits=7)
        rest = x - hi
        mid = lax.reduce_precision(rest, exponent_bits=8, mantissa_bits=7)
        return jnp.stack([hi, mid, rest - mid]).astype(jnp.bfloat16)

    right_partial, first_extra = send_back(
        contributions(data_weight * data_resid),
        jnp.pad(
            request[:, None, :].astype(jnp.float32),
            ((0, 0), (0, 0), (0, block_cells - capacity)),
        ),
    )
    incoming = first_extra[:, :capacity].astype(jnp.int32)
    live_slot = incoming >= 0
    safe_index = jnp.maximum(incoming, 0)
    owner_table = jnp.logical_and(
        safe_index[None] == jnp.arange(blocks_dev, dtype=jnp.int32)[:, None, None],
        live_slot[None],
    )
    owner_table = jnp.broadcast_to(
        owner_table[:, None], (blocks_dev, members, owners, capacity)
    ).astype(jnp.bfloat16)
    reply_table = jnp.logical_and(
        safe_index[:, :, None] == jnp.arange(blocks_dev, dtype=jnp.int32)[None, None, :],
        live_slot[:, :, None],
    ).astype(jnp.bfloat16)

    def gather_cells(rows):
        parts = jnp.einsum(
            "rjoq,sjoqc->src", owner_table, split3(rows), preferred_element_type=jnp.float32
        )
        return (parts[0] + parts[1]) + parts[2]

    def pick_rows(field):
        parts = jnp.einsum(
            "oqr,src->soqc", reply_table, split3(field), preferred_element_type=jnp.float32
        )
        return (parts[0] + parts[1]) + parts[2]

    right_side = gather_cells(right_partial)
    model_step = jnp.zeros(reg_weight.shape, jnp.float32)
    residual = right_side
    direction = right_side
    fetched_dir = None
    norm_now = None
    for iteration in range(ITERS):
        local_norm = jnp.sum(residual * residual)
        replies = pick_rows(residual)
        replies = jnp.concatenate([replies, extra_row(local_norm)], axis=1)
        arrived = lax.all_to_all(replies, "snd", 0, 0, tiled=True)
        norm_next = jnp.sum(arrived[:, capacity, :], axis=0)
        fetched_res = arrived[:, :capacity].reshape(slots, block_cells)
        if iteration == 0:
            fetched_dir = fetched_res
        else:
            ratio = norm_next / norm_now
            direction = residual + ratio * direction
            fetched_dir = fetched_res + ratio * fetched_dir
        norm_now = norm_next
        forward_fetched = sounding_table[:, :, None] * fetched_dir.astype(jnp.bfloat16)[None]
        response = jnp.einsum(
            "spc,fpc->sf", forward_fetched, sens_slots, preferred_element_type=jnp.float32
        )
        partial_gates = jnp.dot(
            response, gate_map, precision=precise, preferred_element_type=jnp.float32
        )
        reg_curve = jnp.sum(reg_weight * direction * direction)
        predicted = lax.psum(partial_gates, "grp")
        weighted = data_weight * predicted
        local_curve = jnp.sum(predicted * weighted) + reg_curve
        image_partial, curve_extra = send_back(contributions(weighted), extra_row(local_curve))
        curvature = jnp.sum(curve_extra, axis=0)
        image_cells = gather_cells(image_partial) + reg_weight * direction
        step_size = norm_now / curvature
        model_step = model_step + step_size * direction
        residual = residual - step_size * image_cells
    return (model_step, residual)


def solution(mesh):
    in_specs = (
        P("snd", None, "grp", None),
        P("grp", None),
        P("snd", None),
        P("snd", None),
        P("snd", None),
        P("snd", None),
        P(),
    )
    out_specs = (P("snd", None), P("snd", None))
    return jax.shard_map(body, mesh=mesh, in_specs=in_specs, out_specs=out_specs, check_vma=False)
```

```python
import jax
import jax.numpy as jnp
from jax import lax
from jax.sharding import PartitionSpec as P

ITERS = 2


precise = lax.Precision.HIGHEST


def body(sensitivity, gate_map, data_resid, data_weight, reg_weight, footprint, block_slot):
    owners = lax.axis_size("snd")
    members = lax.axis_size("grp")
    soundings, per_sounding = footprint.shape
    blocks_dev, block_cells = reg_weight.shape
    entries = soundings * per_sounding
    capacity = members * max(1, 2 * entries // (members * owners))
    blocks = block_slot.shape[0]
    slot_rows = jnp.sum(
        jnp.where(
            footprint[:, :, None] == jnp.arange(blocks, dtype=jnp.int32)[None, None, :],
            block_slot[None, None, :],
            0,
        ),
        axis=2,
    )
    owner_of = slot_rows // blocks_dev
    local_of = slot_rows % blocks_dev
    entry_id = (
        jnp.arange(soundings, dtype=jnp.int32)[:, None] * per_sounding
        + jnp.arange(per_sounding, dtype=jnp.int32)[None, :]
    )
    earlier_same = jnp.logical_and(
        owner_of[:, :, None, None] == owner_of[None, None, :, :],
        entry_id[None, None, :, :] < entry_id[:, :, None, None],
    )
    rank_of = jnp.sum(earlier_same.astype(jnp.int32), axis=(2, 3))
    slots = owners * capacity
    slot_hit = jnp.logical_and(
        owner_of[None, None] == jnp.arange(owners, dtype=jnp.int32)[:, None, None, None],
        rank_of[None, None] == jnp.arange(capacity, dtype=jnp.int32)[None, :, None, None],
    )
    slot_live = jnp.any(slot_hit, axis=(2, 3))
    request = jnp.where(
        slot_live, jnp.sum(jnp.where(slot_hit, local_of[None, None], 0), axis=(2, 3)), -1
    )

    def extra_row(value):
        return jnp.broadcast_to(value.astype(jnp.float32), (owners, 1, block_cells))

    sens_slots = jnp.einsum(
        "oqsk,skfc->foqc",
        slot_hit.astype(sensitivity.dtype),
        sensitivity,
        preferred_element_type=jnp.float32,
    ).astype(sensitivity.dtype).reshape(-1, slots, block_cells)
    slot_sounding = jnp.sum(
        jnp.where(slot_hit, jnp.arange(soundings, dtype=jnp.int32)[:, None], 0), axis=(2, 3)
    ).reshape(slots)
    slot_live = slot_live.reshape(slots)
    sounding_table = jnp.logical_and(
        slot_sounding[None, :] == jnp.arange(soundings, dtype=jnp.int32)[:, None],
        slot_live[None, :],
    ).astype(jnp.bfloat16)

    def contributions(weighted):
        back_freq = jnp.dot(
            weighted, gate_map.T, precision=precise, preferred_element_type=jnp.float32
        ).astype(jnp.bfloat16)
        back_slots = jnp.dot(
            back_freq.T, sounding_table, preferred_element_type=jnp.float32
        ).astype(jnp.bfloat16)
        return jnp.sum(
            sens_slots.astype(jnp.float32) * back_slots.astype(jnp.float32)[:, :, None], axis=0
        )

    def send_back(outgoing, extra):
        outgoing = jnp.concatenate(
            [
                outgoing.reshape(owners, 1, capacity * block_cells),
                extra.reshape(owners, 1, block_cells),
            ],
            axis=2,
        )
        outgoing = jnp.concatenate([outgoing] * members, axis=0)
        returned = lax.all_to_all(outgoing, ("grp", "snd"), 0, 0, tiled=True)
        returned = returned.reshape(members, owners, capacity + 1, block_cells)
        return returned[:, :, :capacity, :], returned[0, :, capacity, :]

    def split3(x):
        hi = lax.reduce_precision(x, exponent_bits=8, mantissa_bits=7)
        rest = x - hi
        mid = lax.reduce_precision(rest, exponent_bits=8, mantissa_bits=7)
        return jnp.stack([hi, mid, rest - mid]).astype(jnp.bfloat16)

    right_partial, first_extra = send_back(
        contributions(data_weight * data_resid),
        jnp.pad(
            request[:, None, :].astype(jnp.float32),
            ((0, 0), (0, 0), (0, block_cells - capacity)),
        ),
    )
    incoming = first_extra[:, :capacity].astype(jnp.int32)
    live_slot = incoming >= 0
    safe_index = jnp.maximum(incoming, 0)
    owner_table = jnp.logical_and(
        safe_index[None] == jnp.arange(blocks_dev, dtype=jnp.int32)[:, None, None],
        live_slot[None],
    )
    owner_table = jnp.broadcast_to(
        owner_table[:, None], (blocks_dev, members, owners, capacity)
    ).astype(jnp.bfloat16)
    reply_table = jnp.logical_and(
        safe_index[:, :, None] == jnp.arange(blocks_dev, dtype=jnp.int32)[None, None, :],
        live_slot[:, :, None],
    ).astype(jnp.bfloat16)

    def gather_cells(rows):
        parts = jnp.einsum(
            "rjoq,sjoqc->src", owner_table, split3(rows), preferred_element_type=jnp.float32
        )
        return (parts[0] + parts[1]) + parts[2]

    def pick_rows(field):
        parts = jnp.einsum(
            "oqr,src->soqc", reply_table, split3(field), preferred_element_type=jnp.float32
        )
        return (parts[0] + parts[1]) + parts[2]

    right_side = gather_cells(right_partial)
    model_step = jnp.zeros(reg_weight.shape, jnp.float32)
    residual = right_side
    direction = right_side
    fetched_dir = None
    norm_now = None
    for iteration in range(ITERS):
        local_norm = jnp.sum(residual * residual)
        replies = pick_rows(residual)
        replies = jnp.concatenate([replies, extra_row(local_norm)], axis=1)
        arrived = lax.all_to_all(replies, "snd", 0, 0, tiled=True)
        norm_next = jnp.sum(arrived[:, capacity, :], axis=0)
        fetched_res = arrived[:, :capacity].reshape(slots, block_cells)
        if iteration == 0:
            fetched_dir = fetched_res
        else:
            ratio = norm_next / norm_now
            direction = residual + ratio * direction
            fetched_dir = fetched_res + ratio * fetched_dir
        norm_now = norm_next
        forward_fetched = sounding_table[:, :, None] * fetched_dir.astype(jnp.bfloat16)[None]
        response = jnp.einsum(
            "spc,fpc->sf", forward_fetched, sens_slots, preferred_element_type=jnp.float32
        )
        partial_gates = jnp.dot(
            response, gate_map, precision=precise, preferred_element_type=jnp.float32
        )
        reg_curve = jnp.sum(reg_weight * direction * direction)
        predicted = lax.psum(partial_gates, "grp")
        weighted = data_weight * predicted
        local_curve = jnp.sum(predicted * weighted) + reg_curve
        image_partial, curve_extra = send_back(contributions(weighted), extra_row(local_curve))
        curvature = jnp.sum(curve_extra, axis=0)
        image_cells = gather_cells(image_partial) + reg_weight * direction
        step_size = norm_now / curvature
        model_step = model_step + step_size * direction
        residual = residual - step_size * image_cells
    return (model_step, residual)


def solution(mesh):
    in_specs = (
        P("snd", None, "grp", None),
        P("grp", None),
        P("snd", None),
        P("snd", None),
        P("snd", None),
        P("snd", None),
        P(),
    )
    out_specs = (P("snd", None), P("snd", None))
    return jax.shard_map(body, mesh=mesh, in_specs=in_specs, out_specs=out_specs, check_vma=False)
```

```python
import jax
import jax.numpy as jnp
from jax import lax
from jax.sharding import PartitionSpec as P

ITERS = 2


precise = lax.Precision.HIGHEST


def body(sensitivity, gate_map, data_resid, data_weight, reg_weight, footprint, block_slot):
    owners = lax.axis_size("snd")
    members = lax.axis_size("grp")
    soundings, per_sounding = footprint.shape
    blocks_dev, block_cells = reg_weight.shape
    entries = soundings * per_sounding
    capacity = members * max(1, 2 * entries // (members * owners))
    blocks = block_slot.shape[0]
    slot_rows = jnp.sum(
        jnp.where(
            footprint[:, :, None] == jnp.arange(blocks, dtype=jnp.int32)[None, None, :],
            block_slot[None, None, :],
            0,
        ),
        axis=2,
    )
    owner_of = slot_rows // blocks_dev
    local_of = slot_rows % blocks_dev
    entry_id = (
        jnp.arange(soundings, dtype=jnp.int32)[:, None] * per_sounding
        + jnp.arange(per_sounding, dtype=jnp.int32)[None, :]
    )
    earlier_same = jnp.logical_and(
        owner_of[:, :, None, None] == owner_of[None, None, :, :],
        entry_id[None, None, :, :] < entry_id[:, :, None, None],
    )
    rank_of = jnp.sum(earlier_same.astype(jnp.int32), axis=(2, 3))
    slots = owners * capacity
    slot_hit = jnp.logical_and(
        owner_of[None, None] == jnp.arange(owners, dtype=jnp.int32)[:, None, None, None],
        rank_of[None, None] == jnp.arange(capacity, dtype=jnp.int32)[None, :, None, None],
    )
    slot_live = jnp.any(slot_hit, axis=(2, 3))
    request = jnp.where(
        slot_live, jnp.sum(jnp.where(slot_hit, local_of[None, None], 0), axis=(2, 3)), -1
    )

    def extra_row(value):
        return jnp.broadcast_to(value.astype(jnp.float32), (owners, 1, block_cells))

    def split3(x):
        hi = lax.reduce_precision(x, exponent_bits=8, mantissa_bits=7)
        rest = x - hi
        mid = lax.reduce_precision(rest, exponent_bits=8, mantissa_bits=7)
        return jnp.stack([hi, mid, rest - mid]).astype(jnp.bfloat16)

    sens_entries = jnp.transpose(sensitivity, (2, 0, 1, 3)).reshape(-1, entries, block_cells)
    slot_table = slot_hit.reshape(slots, entries).astype(jnp.bfloat16)
    entry_table = (
        jnp.arange(entries, dtype=jnp.int32)[None, :] // per_sounding
        == jnp.arange(soundings, dtype=jnp.int32)[:, None]
    ).astype(jnp.bfloat16)

    def to_slots(rows):
        parts = jnp.einsum("pe,sec->spc", slot_table, split3(rows), preferred_element_type=jnp.float32)
        return (parts[0] + parts[1]) + parts[2]

    def contributions(weighted):
        back_freq = jnp.dot(
            weighted, gate_map.T, precision=precise, preferred_element_type=jnp.float32
        ).astype(jnp.bfloat16)
        back_entries = jnp.broadcast_to(
            back_freq.T[:, :, None], (back_freq.shape[1], soundings, per_sounding)
        ).reshape(-1, entries)
        contribution = jnp.sum(
            sens_entries.astype(jnp.float32) * back_entries.astype(jnp.float32)[:, :, None], axis=0
        )
        return to_slots(contribution)

    def send_back(outgoing, extra):
        outgoing = jnp.concatenate(
            [
                outgoing.reshape(owners, 1, capacity * block_cells),
                extra.reshape(owners, 1, block_cells),
            ],
            axis=2,
        )
        outgoing = jnp.concatenate([outgoing] * members, axis=0)
        returned = lax.all_to_all(outgoing, ("grp", "snd"), 0, 0, tiled=True)
        returned = returned.reshape(members, owners, capacity + 1, block_cells)
        return returned[:, :, :capacity, :], returned[0, :, capacity, :]

    right_partial, first_extra = send_back(
        contributions(data_weight * data_resid),
        jnp.pad(
            request[:, None, :].astype(jnp.float32),
            ((0, 0), (0, 0), (0, block_cells - capacity)),
        ),
    )
    incoming = first_extra[:, :capacity].astype(jnp.int32)
    live_slot = incoming >= 0
    safe_index = jnp.maximum(incoming, 0)
    owner_table = jnp.logical_and(
        safe_index[None] == jnp.arange(blocks_dev, dtype=jnp.int32)[:, None, None],
        live_slot[None],
    )
    owner_table = jnp.broadcast_to(
        owner_table[:, None], (blocks_dev, members, owners, capacity)
    ).astype(jnp.bfloat16)
    reply_table = jnp.logical_and(
        safe_index[:, :, None] == jnp.arange(blocks_dev, dtype=jnp.int32)[None, None, :],
        live_slot[:, :, None],
    ).astype(jnp.bfloat16)

    def gather_cells(rows):
        parts = jnp.einsum(
            "rjoq,sjoqc->src", owner_table, split3(rows), preferred_element_type=jnp.float32
        )
        return (parts[0] + parts[1]) + parts[2]

    def pick_rows(field):
        parts = jnp.einsum(
            "oqr,src->soqc", reply_table, split3(field), preferred_element_type=jnp.float32
        )
        return (parts[0] + parts[1]) + parts[2]

    right_side = gather_cells(right_partial)
    model_step = jnp.zeros(reg_weight.shape, jnp.float32)
    residual = right_side
    direction = right_side
    fetched_dir = None
    norm_now = None
    for iteration in range(ITERS):
        local_norm = jnp.sum(residual * residual)
        replies = pick_rows(residual)
        replies = jnp.concatenate([replies, extra_row(local_norm)], axis=1)
        arrived = lax.all_to_all(replies, "snd", 0, 0, tiled=True)
        norm_next = jnp.sum(arrived[:, capacity, :], axis=0)
        fetched_res = arrived[:, :capacity].reshape(slots, block_cells)
        if iteration == 0:
            fetched_dir = fetched_res
        else:
            ratio = norm_next / norm_now
            direction = residual + ratio * direction
            fetched_dir = fetched_res + ratio * fetched_dir
        norm_now = norm_next
        fetched_entries = jnp.dot(
            slot_table.T, fetched_dir.astype(jnp.bfloat16), preferred_element_type=jnp.float32
        ).astype(jnp.bfloat16)
        forward_fetched = entry_table[:, :, None] * fetched_entries[None]
        response = jnp.einsum(
            "sec,fec->sf", forward_fetched, sens_entries, preferred_element_type=jnp.float32
        )
        partial_gates = jnp.dot(
            response, gate_map, precision=precise, preferred_element_type=jnp.float32
        )
        reg_curve = jnp.sum(reg_weight * direction * direction)
        predicted = lax.psum(partial_gates, "grp")
        weighted = data_weight * predicted
        local_curve = jnp.sum(predicted * weighted) + reg_curve
        image_partial, curve_extra = send_back(contributions(weighted), extra_row(local_curve))
        curvature = jnp.sum(curve_extra, axis=0)
        image_cells = gather_cells(image_partial) + reg_weight * direction
        step_size = norm_now / curvature
        model_step = model_step + step_size * direction
        residual = residual - step_size * image_cells
    return (model_step, residual)


def solution(mesh):
    in_specs = (
        P("snd", None, "grp", None),
        P("grp", None),
        P("snd", None),
        P("snd", None),
        P("snd", None),
        P("snd", None),
        P(),
    )
    out_specs = (P("snd", None), P("snd", None))
    return jax.shard_map(body, mesh=mesh, in_specs=in_specs, out_specs=out_specs, check_vma=False)
```

```python
import jax
import jax.numpy as jnp
from jax import lax
from jax.sharding import PartitionSpec as P

ITERS = 2


precise = lax.Precision.HIGHEST


def body(sensitivity, gate_map, data_resid, data_weight, reg_weight, footprint, block_slot):
    owners = lax.axis_size("snd")
    members = lax.axis_size("grp")
    soundings, per_sounding = footprint.shape
    blocks_dev, block_cells = reg_weight.shape
    entries = soundings * per_sounding
    capacity = members * max(1, 2 * entries // (members * owners))
    blocks = block_slot.shape[0]
    slot_rows = jnp.sum(
        jnp.where(
            footprint[:, :, None] == jnp.arange(blocks, dtype=jnp.int32)[None, None, :],
            block_slot[None, None, :],
            0,
        ),
        axis=2,
    )
    owner_of = slot_rows // blocks_dev
    local_of = slot_rows % blocks_dev
    entry_id = (
        jnp.arange(soundings, dtype=jnp.int32)[:, None] * per_sounding
        + jnp.arange(per_sounding, dtype=jnp.int32)[None, :]
    )
    earlier_same = jnp.logical_and(
        owner_of[:, :, None, None] == owner_of[None, None, :, :],
        entry_id[None, None, :, :] < entry_id[:, :, None, None],
    )
    rank_of = jnp.sum(earlier_same.astype(jnp.int32), axis=(2, 3))
    slots = owners * capacity
    slot_hit = jnp.logical_and(
        owner_of[None, None] == jnp.arange(owners, dtype=jnp.int32)[:, None, None, None],
        rank_of[None, None] == jnp.arange(capacity, dtype=jnp.int32)[None, :, None, None],
    )
    slot_live = jnp.any(slot_hit, axis=(2, 3))
    request = jnp.where(
        slot_live, jnp.sum(jnp.where(slot_hit, local_of[None, None], 0), axis=(2, 3)), -1
    )

    def extra_row(value):
        return jnp.broadcast_to(value.astype(jnp.float32)[None, None, :], (owners, 1, block_cells))

    def split3(x):
        hi = lax.reduce_precision(x, exponent_bits=8, mantissa_bits=7)
        rest = x - hi
        mid = lax.reduce_precision(rest, exponent_bits=8, mantissa_bits=7)
        return jnp.stack([hi, mid, rest - mid]).astype(jnp.bfloat16)

    def lane_total(x):
        column = jnp.sum(x, axis=0)
        ones = jnp.ones((column.shape[0], block_cells), jnp.bfloat16)
        parts = jnp.dot(split3(column), ones, preferred_element_type=jnp.float32)
        return (parts[0] + parts[1]) + parts[2]

    sens_slots = jnp.einsum(
        "oqsk,skfc->foqc",
        slot_hit.astype(sensitivity.dtype),
        sensitivity,
        preferred_element_type=jnp.float32,
    ).astype(sensitivity.dtype).reshape(-1, slots, block_cells)
    slot_sounding = jnp.sum(
        jnp.where(slot_hit, jnp.arange(soundings, dtype=jnp.int32)[:, None], 0), axis=(2, 3)
    ).reshape(slots)
    slot_live = slot_live.reshape(slots)
    sounding_table = jnp.logical_and(
        slot_sounding[None, :] == jnp.arange(soundings, dtype=jnp.int32)[:, None],
        slot_live[None, :],
    ).astype(jnp.bfloat16)

    def contributions(weighted):
        back_freq = jnp.dot(
            weighted, gate_map.T, precision=precise, preferred_element_type=jnp.float32
        ).astype(jnp.bfloat16)
        back_slots = jnp.dot(
            back_freq.T, sounding_table, preferred_element_type=jnp.float32
        ).astype(jnp.bfloat16)
        return jnp.sum(
            sens_slots.astype(jnp.float32) * back_slots.astype(jnp.float32)[:, :, None], axis=0
        )

    def send_back(outgoing, extra):
        outgoing = jnp.concatenate(
            [
                outgoing.reshape(owners, 1, capacity * block_cells),
                extra.reshape(owners, 1, block_cells),
            ],
            axis=2,
        )
        outgoing = jnp.concatenate([outgoing] * members, axis=0)
        returned = lax.all_to_all(outgoing, ("grp", "snd"), 0, 0, tiled=True)
        returned = returned.reshape(members, owners, capacity + 1, block_cells)
        return returned[:, :, :capacity, :], returned[0, :, capacity, :]

    right_partial, first_extra = send_back(
        contributions(data_weight * data_resid),
        jnp.pad(
            request[:, None, :].astype(jnp.float32),
            ((0, 0), (0, 0), (0, block_cells - capacity)),
        ),
    )
    incoming = first_extra[:, :capacity].astype(jnp.int32)
    live_slot = incoming >= 0
    safe_index = jnp.maximum(incoming, 0)
    owner_table = jnp.logical_and(
        safe_index[None] == jnp.arange(blocks_dev, dtype=jnp.int32)[:, None, None],
        live_slot[None],
    )
    owner_table = jnp.broadcast_to(
        owner_table[:, None], (blocks_dev, members, owners, capacity)
    ).astype(jnp.bfloat16)
    reply_table = jnp.logical_and(
        safe_index[:, :, None] == jnp.arange(blocks_dev, dtype=jnp.int32)[None, None, :],
        live_slot[:, :, None],
    ).astype(jnp.bfloat16)

    def gather_cells(rows):
        parts = jnp.einsum(
            "rjoq,sjoqc->src", owner_table, split3(rows), preferred_element_type=jnp.float32
        )
        return (parts[0] + parts[1]) + parts[2]

    def pick_rows(field):
        parts = jnp.einsum(
            "oqr,src->soqc", reply_table, split3(field), preferred_element_type=jnp.float32
        )
        return (parts[0] + parts[1]) + parts[2]

    right_side = gather_cells(right_partial)
    model_step = jnp.zeros(reg_weight.shape, jnp.float32)
    residual = right_side
    direction = right_side
    fetched_dir = None
    norm_now = None
    for iteration in range(ITERS):
        local_norm = lane_total(residual * residual)
        replies = pick_rows(residual)
        replies = jnp.concatenate([replies, extra_row(local_norm)], axis=1)
        arrived = lax.all_to_all(replies, "snd", 0, 0, tiled=True)
        norm_next = jnp.sum(arrived[:, capacity, :], axis=0)
        fetched_res = arrived[:, :capacity].reshape(slots, block_cells)
        if iteration == 0:
            fetched_dir = fetched_res
        else:
            ratio = norm_next / norm_now
            direction = residual + ratio * direction
            fetched_dir = fetched_res + ratio * fetched_dir
        norm_now = norm_next
        forward_fetched = sounding_table[:, :, None] * fetched_dir.astype(jnp.bfloat16)[None]
        response = jnp.einsum(
            "spc,fpc->sf", forward_fetched, sens_slots, preferred_element_type=jnp.float32
        )
        partial_gates = jnp.dot(
            response, gate_map, precision=precise, preferred_element_type=jnp.float32
        )
        reg_curve = lane_total(reg_weight * direction * direction)
        predicted = lax.psum(partial_gates, "grp")
        weighted = data_weight * predicted
        local_curve = lane_total(predicted * weighted) + reg_curve
        image_partial, curve_extra = send_back(contributions(weighted), extra_row(local_curve))
        curvature = jnp.sum(curve_extra, axis=0)
        image_cells = gather_cells(image_partial) + reg_weight * direction
        step_size = norm_now / curvature
        model_step = model_step + step_size * direction
        residual = residual - step_size * image_cells
    return (model_step, residual)


def solution(mesh):
    in_specs = (
        P("snd", None, "grp", None),
        P("grp", None),
        P("snd", None),
        P("snd", None),
        P("snd", None),
        P("snd", None),
        P(),
    )
    out_specs = (P("snd", None), P("snd", None))
    return jax.shard_map(body, mesh=mesh, in_specs=in_specs, out_specs=out_specs, check_vma=False)
```

```python
import jax
import jax.numpy as jnp
from jax import lax
from jax.sharding import PartitionSpec as P

ITERS = 2


precise = lax.Precision.HIGHEST


def body(sensitivity, gate_map, data_resid, data_weight, reg_weight, footprint, block_slot):
    owners = lax.axis_size("snd")
    members = lax.axis_size("grp")
    soundings, per_sounding = footprint.shape
    blocks_dev, block_cells = reg_weight.shape
    entries = soundings * per_sounding
    capacity = members * max(1, 2 * entries // (members * owners))
    blocks = block_slot.shape[0]
    slot_rows = jnp.sum(
        jnp.where(
            footprint[None] == jnp.arange(blocks, dtype=jnp.int32)[:, None, None],
            block_slot[:, None, None],
            0,
        ),
        axis=0,
    )
    owner_of = slot_rows // blocks_dev
    local_of = slot_rows % blocks_dev
    entry_id = (
        jnp.arange(soundings, dtype=jnp.int32)[:, None] * per_sounding
        + jnp.arange(per_sounding, dtype=jnp.int32)[None, :]
    )
    earlier_same = jnp.logical_and(
        owner_of[:, :, None, None] == owner_of[None, None, :, :],
        entry_id[:, :, None, None] < entry_id[None, None, :, :],
    )
    rank_of = jnp.sum(earlier_same.astype(jnp.int32), axis=(0, 1))
    slots = owners * capacity
    slot_hit = jnp.logical_and(
        owner_of[:, :, None, None] == jnp.arange(owners, dtype=jnp.int32)[None, None, :, None],
        rank_of[:, :, None, None] == jnp.arange(capacity, dtype=jnp.int32)[None, None, None, :],
    )
    slot_live = jnp.any(slot_hit, axis=(0, 1))
    request = jnp.where(
        slot_live,
        jnp.sum(jnp.where(slot_hit, local_of[:, :, None, None], 0), axis=(0, 1)),
        -1,
    )

    def extra_row(value):
        return jnp.broadcast_to(value.astype(jnp.float32)[None, None, :], (owners, 1, block_cells))

    def split3(x):
        hi = lax.reduce_precision(x, exponent_bits=8, mantissa_bits=7)
        rest = x - hi
        mid = lax.reduce_precision(rest, exponent_bits=8, mantissa_bits=7)
        return jnp.stack([hi, mid, rest - mid]).astype(jnp.bfloat16)

    def lane_total(x):
        column = jnp.sum(x, axis=0)
        ones = jnp.ones((column.shape[0], block_cells), jnp.bfloat16)
        parts = jnp.dot(split3(column), ones, preferred_element_type=jnp.float32)
        return (parts[0] + parts[1]) + parts[2]

    sens_slots = jnp.einsum(
        "skoq,skfc->foqc",
        slot_hit.astype(sensitivity.dtype),
        sensitivity,
        preferred_element_type=jnp.float32,
    ).astype(sensitivity.dtype).reshape(-1, slots, block_cells)
    slot_sounding = jnp.sum(
        jnp.where(slot_hit, jnp.arange(soundings, dtype=jnp.int32)[:, None, None, None], 0),
        axis=(0, 1),
    ).reshape(slots)
    slot_live = slot_live.reshape(slots)
    sounding_table = jnp.logical_and(
        slot_sounding[None, :] == jnp.arange(soundings, dtype=jnp.int32)[:, None],
        slot_live[None, :],
    ).astype(jnp.bfloat16)

    def contributions(weighted):
        back_freq = jnp.dot(
            weighted, gate_map.T, precision=precise, preferred_element_type=jnp.float32
        ).astype(jnp.bfloat16)
        back_slots = jnp.dot(
            back_freq.T, sounding_table, preferred_element_type=jnp.float32
        ).astype(jnp.bfloat16)
        return jnp.sum(
            sens_slots.astype(jnp.float32) * back_slots.astype(jnp.float32)[:, :, None], axis=0
        )

    def send_back(outgoing, extra):
        outgoing = jnp.concatenate(
            [
                outgoing.reshape(owners, 1, capacity * block_cells),
                extra.reshape(owners, 1, block_cells),
            ],
            axis=2,
        )
        outgoing = jnp.concatenate([outgoing] * members, axis=0)
        returned = lax.all_to_all(outgoing, ("grp", "snd"), 0, 0, tiled=True)
        returned = returned.reshape(members, owners, capacity + 1, block_cells)
        return returned[:, :, :capacity, :], returned[0, :, capacity, :]

    right_partial, first_extra = send_back(
        contributions(data_weight * data_resid),
        jnp.pad(
            request[:, None, :].astype(jnp.float32),
            ((0, 0), (0, 0), (0, block_cells - capacity)),
        ),
    )
    incoming = first_extra[:, :capacity].astype(jnp.int32)
    live_slot = incoming >= 0
    safe_index = jnp.maximum(incoming, 0)
    owner_table = jnp.logical_and(
        safe_index[None] == jnp.arange(blocks_dev, dtype=jnp.int32)[:, None, None],
        live_slot[None],
    )
    owner_table = jnp.broadcast_to(
        owner_table[:, None], (blocks_dev, members, owners, capacity)
    ).astype(jnp.bfloat16)
    reply_table = jnp.logical_and(
        safe_index[:, :, None] == jnp.arange(blocks_dev, dtype=jnp.int32)[None, None, :],
        live_slot[:, :, None],
    ).astype(jnp.bfloat16)

    def gather_cells(rows):
        parts = jnp.einsum(
            "rjoq,sjoqc->src", owner_table, split3(rows), preferred_element_type=jnp.float32
        )
        return (parts[0] + parts[1]) + parts[2]

    def pick_rows(field):
        parts = jnp.einsum(
            "oqr,src->soqc", reply_table, split3(field), preferred_element_type=jnp.float32
        )
        return (parts[0] + parts[1]) + parts[2]

    right_side = gather_cells(right_partial)
    model_step = jnp.zeros(reg_weight.shape, jnp.float32)
    residual = right_side
    direction = right_side
    fetched_dir = None
    norm_now = None
    for iteration in range(ITERS):
        local_norm = lane_total(residual * residual)
        replies = pick_rows(residual)
        replies = jnp.concatenate([replies, extra_row(local_norm)], axis=1)
        arrived = lax.all_to_all(replies, "snd", 0, 0, tiled=True)
        norm_next = jnp.sum(arrived[:, capacity, :], axis=0)
        fetched_res = arrived[:, :capacity].reshape(slots, block_cells)
        if iteration == 0:
            fetched_dir = fetched_res
        else:
            ratio = norm_next / norm_now
            direction = residual + ratio * direction
            fetched_dir = fetched_res + ratio * fetched_dir
        norm_now = norm_next
        forward_fetched = sounding_table[:, :, None] * fetched_dir.astype(jnp.bfloat16)[None]
        response = jnp.einsum(
            "spc,fpc->sf", forward_fetched, sens_slots, preferred_element_type=jnp.float32
        )
        partial_gates = jnp.dot(
            response, gate_map, precision=precise, preferred_element_type=jnp.float32
        )
        reg_curve = lane_total(reg_weight * direction * direction)
        predicted = lax.psum(partial_gates, "grp")
        weighted = data_weight * predicted
        local_curve = lane_total(predicted * weighted) + reg_curve
        image_partial, curve_extra = send_back(contributions(weighted), extra_row(local_curve))
        curvature = jnp.sum(curve_extra, axis=0)
        image_cells = gather_cells(image_partial) + reg_weight * direction
        step_size = norm_now / curvature
        model_step = model_step + step_size * direction
        residual = residual - step_size * image_cells
    return (model_step, residual)


def solution(mesh):
    in_specs = (
        P("snd", None, "grp", None),
        P("grp", None),
        P("snd", None),
        P("snd", None),
        P("snd", None),
        P("snd", None),
        P(),
    )
    out_specs = (P("snd", None), P("snd", None))
    return jax.shard_map(body, mesh=mesh, in_specs=in_specs, out_specs=out_specs, check_vma=False)
```

```python
import jax
import jax.numpy as jnp
from jax import lax
from jax.sharding import PartitionSpec as P

ITERS = 2


precise = lax.Precision.HIGHEST


def body(sensitivity, gate_map, data_resid, data_weight, reg_weight, footprint, block_slot):
    owners = lax.axis_size("snd")
    members = lax.axis_size("grp")
    soundings, per_sounding = footprint.shape
    blocks_dev, block_cells = reg_weight.shape
    entries = soundings * per_sounding
    capacity = members * max(1, 2 * entries // (members * owners))
    blocks = block_slot.shape[0]
    slot_rows = jnp.sum(
        jnp.where(
            footprint[:, :, None] == jnp.arange(blocks, dtype=jnp.int32)[None, None, :],
            block_slot[None, None, :],
            0,
        ),
        axis=2,
    )
    owner_of = slot_rows // blocks_dev
    local_of = slot_rows % blocks_dev
    entry_id = (
        jnp.arange(soundings, dtype=jnp.int32)[:, None] * per_sounding
        + jnp.arange(per_sounding, dtype=jnp.int32)[None, :]
    )
    earlier_same = jnp.logical_and(
        owner_of[:, :, None, None] == owner_of[None, None, :, :],
        entry_id[None, None, :, :] < entry_id[:, :, None, None],
    )
    rank_of = jnp.sum(earlier_same.astype(jnp.int32), axis=(2, 3))
    slots = owners * capacity
    slot_hit = jnp.logical_and(
        owner_of[None, None] == jnp.arange(owners, dtype=jnp.int32)[:, None, None, None],
        rank_of[None, None] == jnp.arange(capacity, dtype=jnp.int32)[None, :, None, None],
    )
    slot_live = jnp.any(slot_hit, axis=(2, 3))
    request = jnp.where(
        slot_live, jnp.sum(jnp.where(slot_hit, local_of[None, None], 0), axis=(2, 3)), -1
    )

    def extra_row(value):
        return jnp.broadcast_to(value.astype(jnp.float32)[None, None, :], (owners, 1, block_cells))

    def split3(x):
        hi = lax.reduce_precision(x, exponent_bits=8, mantissa_bits=7)
        rest = x - hi
        mid = lax.reduce_precision(rest, exponent_bits=8, mantissa_bits=7)
        return jnp.stack([hi, mid, rest - mid]).astype(jnp.bfloat16)

    def lane_total(x):
        column = jnp.sum(x, axis=0)
        ones = jnp.ones((column.shape[0], block_cells), jnp.bfloat16)
        parts = jnp.dot(split3(column), ones, preferred_element_type=jnp.float32)
        return (parts[0] + parts[1]) + parts[2]

    sens_slots = jnp.einsum(
        "oqsk,skfc->foqc",
        slot_hit.astype(sensitivity.dtype),
        sensitivity,
        preferred_element_type=jnp.float32,
    ).astype(sensitivity.dtype).reshape(-1, slots, block_cells)
    slot_sounding = jnp.sum(
        jnp.where(slot_hit, jnp.arange(soundings, dtype=jnp.int32)[:, None], 0), axis=(2, 3)
    ).reshape(slots)
    slot_live = slot_live.reshape(slots)
    sounding_table = jnp.logical_and(
        slot_sounding[None, :] == jnp.arange(soundings, dtype=jnp.int32)[:, None],
        slot_live[None, :],
    ).astype(jnp.bfloat16)

    def contributions(weighted):
        back_freq = jnp.dot(
            weighted, gate_map.T, precision=precise, preferred_element_type=jnp.float32
        ).astype(jnp.bfloat16)
        back_slots = jnp.dot(
            back_freq.T, sounding_table, preferred_element_type=jnp.float32
        ).astype(jnp.bfloat16)
        return jnp.sum(
            sens_slots.astype(jnp.float32) * back_slots.astype(jnp.float32)[:, :, None], axis=0
        )

    def send_back(outgoing, extra):
        outgoing = jnp.concatenate(
            [
                outgoing.reshape(owners, 1, capacity * block_cells),
                extra.reshape(owners, 1, block_cells),
            ],
            axis=2,
        )
        outgoing = jnp.concatenate([outgoing] * members, axis=0)
        returned = lax.all_to_all(outgoing, ("grp", "snd"), 0, 0, tiled=True)
        returned = returned.reshape(members, owners, capacity + 1, block_cells)
        return returned[:, :, :capacity, :], returned[0, :, capacity, :]

    def first_contributions(weighted):
        back_freq = jnp.dot(
            weighted, gate_map.T, precision=precise, preferred_element_type=jnp.float32
        ).astype(jnp.bfloat16)
        contribution = jnp.einsum(
            "skfc,sf->skc", sensitivity, back_freq, preferred_element_type=jnp.float32
        )
        parts = jnp.einsum(
            "oqsk,xskc->xoqc",
            slot_hit.astype(jnp.bfloat16),
            split3(contribution),
            preferred_element_type=jnp.float32,
        )
        return ((parts[0] + parts[1]) + parts[2]).reshape(slots, block_cells)

    right_partial, first_extra = send_back(
        first_contributions(data_weight * data_resid),
        jnp.pad(
            request[:, None, :].astype(jnp.float32),
            ((0, 0), (0, 0), (0, block_cells - capacity)),
        ),
    )
    incoming = first_extra[:, :capacity].astype(jnp.int32)
    live_slot = incoming >= 0
    safe_index = jnp.maximum(incoming, 0)
    owner_table = jnp.logical_and(
        safe_index[None] == jnp.arange(blocks_dev, dtype=jnp.int32)[:, None, None],
        live_slot[None],
    )
    owner_table = jnp.broadcast_to(
        owner_table[:, None], (blocks_dev, members, owners, capacity)
    ).astype(jnp.bfloat16)
    reply_table = jnp.logical_and(
        safe_index[:, :, None] == jnp.arange(blocks_dev, dtype=jnp.int32)[None, None, :],
        live_slot[:, :, None],
    ).astype(jnp.bfloat16)

    def gather_cells(rows):
        parts = jnp.einsum(
            "rjoq,sjoqc->src", owner_table, split3(rows), preferred_element_type=jnp.float32
        )
        return (parts[0] + parts[1]) + parts[2]

    def pick_rows(field):
        parts = jnp.einsum(
            "oqr,src->soqc", reply_table, split3(field), preferred_element_type=jnp.float32
        )
        return (parts[0] + parts[1]) + parts[2]

    right_side = gather_cells(right_partial)
    model_step = jnp.zeros(reg_weight.shape, jnp.float32)
    residual = right_side
    direction = right_side
    fetched_dir = None
    norm_now = None
    for iteration in range(ITERS):
        local_norm = lane_total(residual * residual)
        replies = pick_rows(residual)
        replies = jnp.concatenate([replies, extra_row(local_norm)], axis=1)
        arrived = lax.all_to_all(replies, "snd", 0, 0, tiled=True)
        norm_next = jnp.sum(arrived[:, capacity, :], axis=0)
        fetched_res = arrived[:, :capacity].reshape(slots, block_cells)
        if iteration == 0:
            fetched_dir = fetched_res
        else:
            ratio = norm_next / norm_now
            direction = residual + ratio * direction
            fetched_dir = fetched_res + ratio * fetched_dir
        norm_now = norm_next
        forward_fetched = sounding_table[:, :, None] * fetched_dir.astype(jnp.bfloat16)[None]
        response = jnp.einsum(
            "spc,fpc->sf", forward_fetched, sens_slots, preferred_element_type=jnp.float32
        )
        partial_gates = jnp.dot(
            response, gate_map, precision=precise, preferred_element_type=jnp.float32
        )
        reg_curve = lane_total(reg_weight * direction * direction)
        predicted = lax.psum(partial_gates, "grp")
        weighted = data_weight * predicted
        local_curve = lane_total(predicted * weighted) + reg_curve
        image_partial, curve_extra = send_back(contributions(weighted), extra_row(local_curve))
        curvature = jnp.sum(curve_extra, axis=0)
        image_cells = gather_cells(image_partial) + reg_weight * direction
        step_size = norm_now / curvature
        model_step = model_step + step_size * direction
        residual = residual - step_size * image_cells
    return (model_step, residual)


def solution(mesh):
    in_specs = (
        P("snd", None, "grp", None),
        P("grp", None),
        P("snd", None),
        P("snd", None),
        P("snd", None),
        P("snd", None),
        P(),
    )
    out_specs = (P("snd", None), P("snd", None))
    return jax.shard_map(body, mesh=mesh, in_specs=in_specs, out_specs=out_specs, check_vma=False)
```

```python
import jax
import jax.numpy as jnp
from jax import lax
from jax.sharding import PartitionSpec as P

ITERS = 2


precise = lax.Precision.HIGHEST


def body(sensitivity, gate_map, data_resid, data_weight, reg_weight, footprint, block_slot):
    owners = lax.axis_size("snd")
    members = lax.axis_size("grp")
    soundings, per_sounding = footprint.shape
    blocks_dev, block_cells = reg_weight.shape
    entries = soundings * per_sounding
    capacity = members * max(1, 2 * entries // (members * owners))
    blocks = block_slot.shape[0]
    digits = jnp.stack([block_slot // 64, block_slot % 64], axis=1).astype(jnp.bfloat16)
    picked = jnp.dot(
        (footprint.reshape(entries, 1) == jnp.arange(blocks, dtype=jnp.int32)[None, :]).astype(
            jnp.bfloat16
        ),
        digits,
        preferred_element_type=jnp.float32,
    ).astype(jnp.int32)
    slot_rows = (picked[:, 0] * 64 + picked[:, 1]).reshape(soundings, per_sounding)
    owner_of = slot_rows // blocks_dev
    local_of = slot_rows % blocks_dev
    entry_id = (
        jnp.arange(soundings, dtype=jnp.int32)[:, None] * per_sounding
        + jnp.arange(per_sounding, dtype=jnp.int32)[None, :]
    )
    earlier_same = jnp.logical_and(
        owner_of[:, :, None, None] == owner_of[None, None, :, :],
        entry_id[None, None, :, :] < entry_id[:, :, None, None],
    )
    rank_of = jnp.sum(earlier_same.astype(jnp.int32), axis=(2, 3))
    slots = owners * capacity
    slot_hit = jnp.logical_and(
        owner_of[None, None] == jnp.arange(owners, dtype=jnp.int32)[:, None, None, None],
        rank_of[None, None] == jnp.arange(capacity, dtype=jnp.int32)[None, :, None, None],
    )
    slot_live = jnp.any(slot_hit, axis=(2, 3))
    request = jnp.where(
        slot_live, jnp.sum(jnp.where(slot_hit, local_of[None, None], 0), axis=(2, 3)), -1
    )

    def extra_row(value):
        return jnp.broadcast_to(value.astype(jnp.float32)[None, None, :], (owners, 1, block_cells))

    def split3(x):
        hi = lax.reduce_precision(x, exponent_bits=8, mantissa_bits=7)
        rest = x - hi
        mid = lax.reduce_precision(rest, exponent_bits=8, mantissa_bits=7)
        return jnp.stack([hi, mid, rest - mid]).astype(jnp.bfloat16)

    def lane_total(x):
        column = jnp.sum(x, axis=0)
        ones = jnp.ones((column.shape[0], block_cells), jnp.bfloat16)
        parts = jnp.dot(split3(column), ones, preferred_element_type=jnp.float32)
        return (parts[0] + parts[1]) + parts[2]

    sens_slots = jnp.einsum(
        "oqsk,skfc->foqc",
        slot_hit.astype(sensitivity.dtype),
        sensitivity,
        preferred_element_type=jnp.float32,
    ).astype(sensitivity.dtype).reshape(-1, slots, block_cells)
    slot_sounding = jnp.sum(
        jnp.where(slot_hit, jnp.arange(soundings, dtype=jnp.int32)[:, None], 0), axis=(2, 3)
    ).reshape(slots)
    slot_live = slot_live.reshape(slots)
    sounding_table = jnp.logical_and(
        slot_sounding[None, :] == jnp.arange(soundings, dtype=jnp.int32)[:, None],
        slot_live[None, :],
    ).astype(jnp.bfloat16)

    def contributions(weighted):
        back_freq = jnp.dot(
            weighted, gate_map.T, precision=precise, preferred_element_type=jnp.float32
        ).astype(jnp.bfloat16)
        back_slots = jnp.dot(
            back_freq.T, sounding_table, preferred_element_type=jnp.float32
        ).astype(jnp.bfloat16)
        return jnp.sum(
            sens_slots.astype(jnp.float32) * back_slots.astype(jnp.float32)[:, :, None], axis=0
        )

    def send_back(outgoing, extra):
        outgoing = jnp.concatenate(
            [
                outgoing.reshape(owners, 1, capacity * block_cells),
                extra.reshape(owners, 1, block_cells),
            ],
            axis=2,
        )
        outgoing = jnp.concatenate([outgoing] * members, axis=0)
        returned = lax.all_to_all(outgoing, ("grp", "snd"), 0, 0, tiled=True)
        returned = returned.reshape(members, owners, capacity + 1, block_cells)
        return returned[:, :, :capacity, :], returned[0, :, capacity, :]

    def first_contributions(weighted):
        back_freq = jnp.dot(
            weighted, gate_map.T, precision=precise, preferred_element_type=jnp.float32
        ).astype(jnp.bfloat16)
        contribution = jnp.einsum(
            "skfc,sf->skc", sensitivity, back_freq, preferred_element_type=jnp.float32
        )
        parts = jnp.einsum(
            "oqsk,xskc->xoqc",
            slot_hit.astype(jnp.bfloat16),
            split3(contribution),
            preferred_element_type=jnp.float32,
        )
        return ((parts[0] + parts[1]) + parts[2]).reshape(slots, block_cells)

    right_partial, first_extra = send_back(
        first_contributions(data_weight * data_resid),
        jnp.pad(
            request[:, None, :].astype(jnp.float32),
            ((0, 0), (0, 0), (0, block_cells - capacity)),
        ),
    )
    incoming = first_extra[:, :capacity].astype(jnp.int32)
    live_slot = incoming >= 0
    safe_index = jnp.maximum(incoming, 0)
    owner_table = jnp.logical_and(
        safe_index[None] == jnp.arange(blocks_dev, dtype=jnp.int32)[:, None, None],
        live_slot[None],
    )
    owner_table = jnp.broadcast_to(
        owner_table[:, None], (blocks_dev, members, owners, capacity)
    ).astype(jnp.bfloat16)
    reply_table = jnp.logical_and(
        safe_index[:, :, None] == jnp.arange(blocks_dev, dtype=jnp.int32)[None, None, :],
        live_slot[:, :, None],
    ).astype(jnp.bfloat16)

    def gather_cells(rows):
        parts = jnp.einsum(
            "rjoq,sjoqc->src", owner_table, split3(rows), preferred_element_type=jnp.float32
        )
        return (parts[0] + parts[1]) + parts[2]

    def pick_rows(field):
        parts = jnp.einsum(
            "oqr,src->soqc", reply_table, split3(field), preferred_element_type=jnp.float32
        )
        return (parts[0] + parts[1]) + parts[2]

    right_side = gather_cells(right_partial)
    model_step = jnp.zeros(reg_weight.shape, jnp.float32)
    residual = right_side
    direction = right_side
    fetched_dir = None
    norm_now = None
    for iteration in range(ITERS):
        local_norm = lane_total(residual * residual)
        replies = pick_rows(residual)
        replies = jnp.concatenate([replies, extra_row(local_norm)], axis=1)
        arrived = lax.all_to_all(replies, "snd", 0, 0, tiled=True)
        norm_next = jnp.sum(arrived[:, capacity, :], axis=0)
        fetched_res = arrived[:, :capacity].reshape(slots, block_cells)
        if iteration == 0:
            fetched_dir = fetched_res
        else:
            ratio = norm_next / norm_now
            direction = residual + ratio * direction
            fetched_dir = fetched_res + ratio * fetched_dir
        norm_now = norm_next
        forward_fetched = sounding_table[:, :, None] * fetched_dir.astype(jnp.bfloat16)[None]
        response = jnp.einsum(
            "spc,fpc->sf", forward_fetched, sens_slots, preferred_element_type=jnp.float32
        )
        partial_gates = jnp.dot(
            response, gate_map, precision=precise, preferred_element_type=jnp.float32
        )
        reg_curve = lane_total(reg_weight * direction * direction)
        predicted = lax.psum(partial_gates, "grp")
        weighted = data_weight * predicted
        local_curve = lane_total(predicted * weighted) + reg_curve
        image_partial, curve_extra = send_back(contributions(weighted), extra_row(local_curve))
        curvature = jnp.sum(curve_extra, axis=0)
        image_cells = gather_cells(image_partial) + reg_weight * direction
        step_size = norm_now / curvature
        model_step = model_step + step_size * direction
        residual = residual - step_size * image_cells
    return (model_step, residual)


def solution(mesh):
    in_specs = (
        P("snd", None, "grp", None),
        P("grp", None),
        P("snd", None),
        P("snd", None),
        P("snd", None),
        P("snd", None),
        P(),
    )
    out_specs = (P("snd", None), P("snd", None))
    return jax.shard_map(body, mesh=mesh, in_specs=in_specs, out_specs=out_specs, check_vma=False)
```

```python
import jax
import jax.numpy as jnp
from jax import lax
from jax.sharding import PartitionSpec as P

ITERS = 2


precise = lax.Precision.HIGHEST


def body(sensitivity, gate_map, data_resid, data_weight, reg_weight, footprint, block_slot):
    owners = lax.axis_size("snd")
    members = lax.axis_size("grp")
    soundings, per_sounding = footprint.shape
    blocks_dev, block_cells = reg_weight.shape
    entries = soundings * per_sounding
    capacity = members * max(1, 2 * entries // (members * owners))
    blocks = block_slot.shape[0]
    slot_rows = jnp.sum(
        jnp.where(
            footprint[:, :, None] == jnp.arange(blocks, dtype=jnp.int32)[None, None, :],
            block_slot[None, None, :],
            0,
        ),
        axis=2,
    )
    owner_of = slot_rows // blocks_dev
    local_of = slot_rows % blocks_dev
    entry_id = (
        jnp.arange(soundings, dtype=jnp.int32)[:, None] * per_sounding
        + jnp.arange(per_sounding, dtype=jnp.int32)[None, :]
    )
    earlier_same = jnp.logical_and(
        owner_of[:, :, None, None] == owner_of[None, None, :, :],
        entry_id[None, None, :, :] < entry_id[:, :, None, None],
    )
    rank_of = jnp.sum(earlier_same.astype(jnp.int32), axis=(2, 3))
    slots = owners * capacity
    slot_hit = jnp.logical_and(
        owner_of[None, None] == jnp.arange(owners, dtype=jnp.int32)[:, None, None, None],
        rank_of[None, None] == jnp.arange(capacity, dtype=jnp.int32)[None, :, None, None],
    )
    slot_live = jnp.any(slot_hit, axis=(2, 3))
    request = jnp.where(
        slot_live, jnp.sum(jnp.where(slot_hit, local_of[None, None], 0), axis=(2, 3)), -1
    )

    def extra_row(value):
        return jnp.broadcast_to(value.astype(jnp.float32)[None, None, :], (owners, 1, block_cells))

    def split3(x):
        hi = lax.reduce_precision(x, exponent_bits=8, mantissa_bits=7)
        rest = x - hi
        mid = lax.reduce_precision(rest, exponent_bits=8, mantissa_bits=7)
        return jnp.stack([hi, mid, rest - mid]).astype(jnp.bfloat16)

    def lane_total(x):
        column = jnp.sum(x, axis=0)
        ones = jnp.ones((column.shape[0], block_cells), jnp.bfloat16)
        parts = jnp.dot(split3(column), ones, preferred_element_type=jnp.float32)
        return (parts[0] + parts[1]) + parts[2]

    sens_slots = jnp.einsum(
        "oqsk,skfc->foqc",
        slot_hit.astype(sensitivity.dtype),
        sensitivity,
        preferred_element_type=jnp.float32,
    ).astype(sensitivity.dtype).reshape(-1, slots, block_cells)
    slot_sounding = jnp.sum(
        jnp.where(slot_hit, jnp.arange(soundings, dtype=jnp.int32)[:, None], 0), axis=(2, 3)
    ).reshape(slots)
    slot_live = slot_live.reshape(slots)
    sounding_table = jnp.logical_and(
        slot_sounding[None, :] == jnp.arange(soundings, dtype=jnp.int32)[:, None],
        slot_live[None, :],
    ).astype(jnp.bfloat16)

    def contributions(weighted):
        back_freq = jnp.dot(
            weighted, gate_map.T, precision=precise, preferred_element_type=jnp.float32
        ).astype(jnp.bfloat16)
        back_slots = jnp.dot(
            back_freq.T, sounding_table, preferred_element_type=jnp.float32
        ).astype(jnp.bfloat16)
        return jnp.sum(
            sens_slots.astype(jnp.float32) * back_slots.astype(jnp.float32)[:, :, None], axis=0
        )

    def send_back(outgoing, extra):
        outgoing = jnp.concatenate(
            [
                outgoing.reshape(owners, 1, capacity * block_cells),
                extra.reshape(owners, 1, block_cells),
            ],
            axis=2,
        )
        outgoing = jnp.concatenate([outgoing] * members, axis=0)
        returned = lax.all_to_all(outgoing, ("grp", "snd"), 0, 0, tiled=True)
        returned = returned.reshape(members, owners, capacity + 1, block_cells)
        return returned[:, :, :capacity, :], returned[0, :, capacity, :]

    def first_contributions(weighted):
        back_freq = jnp.dot(
            weighted, gate_map.T, precision=precise, preferred_element_type=jnp.float32
        ).astype(jnp.bfloat16)
        contribution = jnp.einsum(
            "skfc,sf->skc", sensitivity, back_freq, preferred_element_type=jnp.float32
        )
        parts = jnp.einsum(
            "oqsk,xskc->xoqc",
            slot_hit.astype(jnp.bfloat16),
            split3(contribution),
            preferred_element_type=jnp.float32,
        )
        return ((parts[0] + parts[1]) + parts[2]).reshape(slots, block_cells)

    right_partial, first_extra = send_back(
        first_contributions(data_weight * data_resid),
        jnp.pad(
            request[:, None, :].astype(jnp.float32),
            ((0, 0), (0, 0), (0, block_cells - capacity)),
        ),
    )
    incoming = first_extra[:, :capacity].astype(jnp.int32)
    live_slot = incoming >= 0
    safe_index = jnp.maximum(incoming, 0)
    owner_table = jnp.logical_and(
        safe_index[None] == jnp.arange(blocks_dev, dtype=jnp.int32)[:, None, None],
        live_slot[None],
    )
    owner_table = jnp.broadcast_to(
        owner_table[:, None], (blocks_dev, members, owners, capacity)
    ).astype(jnp.bfloat16)
    reply_table = jnp.logical_and(
        safe_index[:, :, None] == jnp.arange(blocks_dev, dtype=jnp.int32)[None, None, :],
        live_slot[:, :, None],
    ).astype(jnp.bfloat16)

    def gather_cells(rows):
        parts = jnp.einsum(
            "rjoq,sjoqc->src", owner_table, split3(rows), preferred_element_type=jnp.float32
        )
        return (parts[0] + parts[1]) + parts[2]

    def pick_rows(field):
        parts = jnp.einsum(
            "oqr,src->soqc", reply_table, split3(field), preferred_element_type=jnp.float32
        )
        return (parts[0] + parts[1]) + parts[2]

    reply_from_slots = jnp.einsum(
        "oqr,rjpt->oqjpt", reply_table, owner_table, preferred_element_type=jnp.float32
    ).astype(jnp.bfloat16)

    def reply_cells(rows):
        parts = jnp.einsum(
            "oqjpt,sjptc->soqc", reply_from_slots, split3(rows), preferred_element_type=jnp.float32
        )
        return (parts[0] + parts[1]) + parts[2]

    right_side = gather_cells(right_partial)
    replies = reply_cells(right_partial)
    model_step = jnp.zeros(reg_weight.shape, jnp.float32)
    residual = right_side
    direction = right_side
    fetched_dir = None
    norm_now = None
    for iteration in range(ITERS):
        local_norm = lane_total(residual * residual)
        sent = replies
        replies = jnp.concatenate([replies, extra_row(local_norm)], axis=1)
        arrived = lax.all_to_all(replies, "snd", 0, 0, tiled=True)
        norm_next = jnp.sum(arrived[:, capacity, :], axis=0)
        fetched_res = arrived[:, :capacity].reshape(slots, block_cells)
        if iteration == 0:
            fetched_dir = fetched_res
        else:
            ratio = norm_next / norm_now
            direction = residual + ratio * direction
            fetched_dir = fetched_res + ratio * fetched_dir
        norm_now = norm_next
        forward_fetched = sounding_table[:, :, None] * fetched_dir.astype(jnp.bfloat16)[None]
        response = jnp.einsum(
            "spc,fpc->sf", forward_fetched, sens_slots, preferred_element_type=jnp.float32
        )
        partial_gates = jnp.dot(
            response, gate_map, precision=precise, preferred_element_type=jnp.float32
        )
        reg_curve = lane_total(reg_weight * direction * direction)
        predicted = lax.psum(partial_gates, "grp")
        weighted = data_weight * predicted
        local_curve = lane_total(predicted * weighted) + reg_curve
        image_partial, curve_extra = send_back(contributions(weighted), extra_row(local_curve))
        curvature = jnp.sum(curve_extra, axis=0)
        image_cells = gather_cells(image_partial) + reg_weight * direction
        step_size = norm_now / curvature
        model_step = model_step + step_size * direction
        residual = residual - step_size * image_cells
        if iteration + 1 < ITERS:
            reply_image = reply_cells(image_partial) + pick_rows(reg_weight * direction)
            replies = sent - step_size * reply_image
    return (model_step, residual)


def solution(mesh):
    in_specs = (
        P("snd", None, "grp", None),
        P("grp", None),
        P("snd", None),
        P("snd", None),
        P("snd", None),
        P("snd", None),
        P(),
    )
    out_specs = (P("snd", None), P("snd", None))
    return jax.shard_map(body, mesh=mesh, in_specs=in_specs, out_specs=out_specs, check_vma=False)
```

```python
import jax
import jax.numpy as jnp
from jax import lax
from jax.sharding import PartitionSpec as P

ITERS = 2


precise = lax.Precision.HIGHEST


def body(sensitivity, gate_map, data_resid, data_weight, reg_weight, footprint, block_slot):
    owners = lax.axis_size("snd")
    members = lax.axis_size("grp")
    soundings, per_sounding = footprint.shape
    blocks_dev, block_cells = reg_weight.shape
    entries = soundings * per_sounding
    capacity = members * max(1, 2 * entries // (members * owners))
    blocks = block_slot.shape[0]
    slot_rows = jnp.sum(
        jnp.where(
            footprint[:, :, None] == jnp.arange(blocks, dtype=jnp.int32)[None, None, :],
            block_slot[None, None, :],
            0,
        ),
        axis=2,
    )
    owner_of = slot_rows // blocks_dev
    local_of = slot_rows % blocks_dev
    entry_id = (
        jnp.arange(soundings, dtype=jnp.int32)[:, None] * per_sounding
        + jnp.arange(per_sounding, dtype=jnp.int32)[None, :]
    )
    earlier_same = jnp.logical_and(
        owner_of[:, :, None, None] == owner_of[None, None, :, :],
        entry_id[None, None, :, :] < entry_id[:, :, None, None],
    )
    rank_of = jnp.sum(earlier_same.astype(jnp.int32), axis=(2, 3))
    slots = owners * capacity
    slot_hit = jnp.logical_and(
        owner_of[None, None] == jnp.arange(owners, dtype=jnp.int32)[:, None, None, None],
        rank_of[None, None] == jnp.arange(capacity, dtype=jnp.int32)[None, :, None, None],
    )
    slot_live = jnp.any(slot_hit, axis=(2, 3))
    request = jnp.where(
        slot_live, jnp.sum(jnp.where(slot_hit, local_of[None, None], 0), axis=(2, 3)), -1
    )

    def extra_row(value):
        return jnp.broadcast_to(value.astype(jnp.float32)[None, None, :], (owners, 1, block_cells))

    def split3(x):
        hi = lax.reduce_precision(x, exponent_bits=8, mantissa_bits=7)
        rest = x - hi
        mid = lax.reduce_precision(rest, exponent_bits=8, mantissa_bits=7)
        return jnp.stack([hi, mid, rest - mid]).astype(jnp.bfloat16)

    def lane_total(x):
        column = jnp.sum(x, axis=0)
        ones = jnp.ones((column.shape[0], block_cells), jnp.bfloat16)
        parts = jnp.dot(split3(column), ones, preferred_element_type=jnp.float32)
        return (parts[0] + parts[1]) + parts[2]

    sens_slots = jnp.einsum(
        "oqsk,skfc->foqc",
        slot_hit.astype(sensitivity.dtype),
        sensitivity,
        preferred_element_type=jnp.float32,
    ).astype(sensitivity.dtype).reshape(-1, slots, block_cells)
    slot_sounding = jnp.sum(
        jnp.where(slot_hit, jnp.arange(soundings, dtype=jnp.int32)[:, None], 0), axis=(2, 3)
    ).reshape(slots)
    slot_live = slot_live.reshape(slots)
    sounding_table = jnp.logical_and(
        slot_sounding[None, :] == jnp.arange(soundings, dtype=jnp.int32)[:, None],
        slot_live[None, :],
    ).astype(jnp.bfloat16)

    def contributions(weighted):
        back_freq = jnp.dot(
            weighted, gate_map.T, precision=precise, preferred_element_type=jnp.float32
        ).astype(jnp.bfloat16)
        back_slots = jnp.dot(
            back_freq.T, sounding_table, preferred_element_type=jnp.float32
        ).astype(jnp.bfloat16)
        return jnp.sum(
            sens_slots.astype(jnp.float32) * back_slots.astype(jnp.float32)[:, :, None], axis=0
        )

    def send_back(outgoing, extra):
        outgoing = jnp.concatenate(
            [
                outgoing.reshape(owners, 1, capacity * block_cells),
                extra.reshape(owners, 1, block_cells),
            ],
            axis=2,
        )
        outgoing = jnp.concatenate([outgoing] * members, axis=0)
        returned = lax.all_to_all(outgoing, ("grp", "snd"), 0, 0, tiled=True)
        returned = returned.reshape(members, owners, capacity + 1, block_cells)
        return returned[:, :, :capacity, :], returned[0, :, capacity, :]

    def first_contributions(weighted):
        back_freq = jnp.sum(weighted[:, None, :] * gate_map[None, :, :], axis=2).astype(jnp.bfloat16)
        contribution = jnp.einsum(
            "skfc,sf->skc", sensitivity, back_freq, preferred_element_type=jnp.float32
        )
        parts = jnp.einsum(
            "oqsk,xskc->xoqc",
            slot_hit.astype(jnp.bfloat16),
            split3(contribution),
            preferred_element_type=jnp.float32,
        )
        return ((parts[0] + parts[1]) + parts[2]).reshape(slots, block_cells)

    right_partial, first_extra = send_back(
        first_contributions(data_weight * data_resid),
        jnp.pad(
            request[:, None, :].astype(jnp.float32),
            ((0, 0), (0, 0), (0, block_cells - capacity)),
        ),
    )
    incoming = first_extra[:, :capacity].astype(jnp.int32)
    live_slot = incoming >= 0
    safe_index = jnp.maximum(incoming, 0)
    owner_table = jnp.logical_and(
        safe_index[None] == jnp.arange(blocks_dev, dtype=jnp.int32)[:, None, None],
        live_slot[None],
    )
    owner_table = jnp.broadcast_to(
        owner_table[:, None], (blocks_dev, members, owners, capacity)
    ).astype(jnp.bfloat16)
    reply_table = jnp.logical_and(
        safe_index[:, :, None] == jnp.arange(blocks_dev, dtype=jnp.int32)[None, None, :],
        live_slot[:, :, None],
    ).astype(jnp.bfloat16)

    def gather_cells(rows):
        parts = jnp.einsum(
            "rjoq,sjoqc->src", owner_table, split3(rows), preferred_element_type=jnp.float32
        )
        return (parts[0] + parts[1]) + parts[2]

    def pick_rows(field):
        parts = jnp.einsum(
            "oqr,src->soqc", reply_table, split3(field), preferred_element_type=jnp.float32
        )
        return (parts[0] + parts[1]) + parts[2]

    right_side = gather_cells(right_partial)
    model_step = jnp.zeros(reg_weight.shape, jnp.float32)
    residual = right_side
    direction = right_side
    fetched_dir = None
    norm_now = None
    for iteration in range(ITERS):
        local_norm = lane_total(residual * residual)
        replies = pick_rows(residual)
        replies = jnp.concatenate([replies, extra_row(local_norm)], axis=1)
        arrived = lax.all_to_all(replies, "snd", 0, 0, tiled=True)
        norm_next = jnp.sum(arrived[:, capacity, :], axis=0)
        fetched_res = arrived[:, :capacity].reshape(slots, block_cells)
        if iteration == 0:
            fetched_dir = fetched_res
        else:
            ratio = norm_next / norm_now
            direction = residual + ratio * direction
            fetched_dir = fetched_res + ratio * fetched_dir
        norm_now = norm_next
        forward_fetched = sounding_table[:, :, None] * fetched_dir.astype(jnp.bfloat16)[None]
        response = jnp.einsum(
            "spc,fpc->sf", forward_fetched, sens_slots, preferred_element_type=jnp.float32
        )
        partial_gates = jnp.dot(
            response, gate_map, precision=precise, preferred_element_type=jnp.float32
        )
        reg_column = jnp.sum(reg_weight * direction * direction, axis=0)
        predicted = lax.psum(partial_gates, "grp")
        weighted = data_weight * predicted
        data_column = jnp.sum(predicted * weighted, axis=0)
        local_curve = lane_total(
            jnp.stack([reg_column, jnp.pad(data_column, (0, block_cells - data_column.shape[0]))])
        )
        image_partial, curve_extra = send_back(contributions(weighted), extra_row(local_curve))
        curvature = jnp.sum(curve_extra, axis=0)
        image_cells = gather_cells(image_partial) + reg_weight * direction
        step_size = norm_now / curvature
        model_step = model_step + step_size * direction
        residual = residual - step_size * image_cells
    return (model_step, residual)


def solution(mesh):
    in_specs = (
        P("snd", None, "grp", None),
        P("grp", None),
        P("snd", None),
        P("snd", None),
        P("snd", None),
        P("snd", None),
        P(),
    )
    out_specs = (P("snd", None), P("snd", None))
    return jax.shard_map(body, mesh=mesh, in_specs=in_specs, out_specs=out_specs, check_vma=False)
```

```python
import jax
import jax.numpy as jnp
from jax import lax
from jax.sharding import PartitionSpec as P

ITERS = 2


precise = lax.Precision.HIGHEST


def body(sensitivity, gate_map, data_resid, data_weight, reg_weight, footprint, block_slot):
    owners = lax.axis_size("snd")
    members = lax.axis_size("grp")
    soundings, per_sounding = footprint.shape
    blocks_dev, block_cells = reg_weight.shape
    entries = soundings * per_sounding
    capacity = members * max(1, 2 * entries // (members * owners))
    blocks = block_slot.shape[0]
    slot_rows = jnp.sum(
        jnp.where(
            footprint[:, :, None] == jnp.arange(blocks, dtype=jnp.int32)[None, None, :],
            block_slot[None, None, :],
            0,
        ),
        axis=2,
    )
    owner_of = slot_rows // blocks_dev
    local_of = slot_rows % blocks_dev
    entry_id = (
        jnp.arange(soundings, dtype=jnp.int32)[:, None] * per_sounding
        + jnp.arange(per_sounding, dtype=jnp.int32)[None, :]
    )
    earlier_same = jnp.logical_and(
        owner_of[:, :, None, None] == owner_of[None, None, :, :],
        entry_id[None, None, :, :] < entry_id[:, :, None, None],
    )
    rank_of = jnp.sum(earlier_same.astype(jnp.int32), axis=(2, 3))
    slots = owners * capacity
    slot_hit = jnp.logical_and(
        owner_of[None, None] == jnp.arange(owners, dtype=jnp.int32)[:, None, None, None],
        rank_of[None, None] == jnp.arange(capacity, dtype=jnp.int32)[None, :, None, None],
    )
    slot_live = jnp.any(slot_hit, axis=(2, 3))
    request = jnp.where(
        slot_live, jnp.sum(jnp.where(slot_hit, local_of[None, None], 0), axis=(2, 3)), -1
    )

    def extra_row(value):
        return jnp.broadcast_to(value.astype(jnp.float32)[None, None, :], (owners, 1, block_cells))

    def split3(x):
        hi = lax.reduce_precision(x, exponent_bits=8, mantissa_bits=7)
        rest = x - hi
        mid = lax.reduce_precision(rest, exponent_bits=8, mantissa_bits=7)
        return jnp.stack([hi, mid, rest - mid]).astype(jnp.bfloat16)

    def lane_total(x):
        column = jnp.sum(x, axis=0)
        ones = jnp.ones((column.shape[0], block_cells), jnp.bfloat16)
        parts = jnp.dot(split3(column), ones, preferred_element_type=jnp.float32)
        return (parts[0] + parts[1]) + parts[2]

    sens_slots = jnp.einsum(
        "oqsk,skfc->foqc",
        slot_hit.astype(sensitivity.dtype),
        sensitivity,
        preferred_element_type=jnp.float32,
    ).astype(sensitivity.dtype).reshape(-1, slots, block_cells)
    slot_sounding = jnp.sum(
        jnp.where(slot_hit, jnp.arange(soundings, dtype=jnp.int32)[:, None], 0), axis=(2, 3)
    ).reshape(slots)
    slot_live = slot_live.reshape(slots)
    sounding_table = jnp.logical_and(
        slot_sounding[None, :] == jnp.arange(soundings, dtype=jnp.int32)[:, None],
        slot_live[None, :],
    ).astype(jnp.bfloat16)

    def contributions(weighted):
        back_freq = jnp.dot(
            weighted, gate_map.T, precision=precise, preferred_element_type=jnp.float32
        ).astype(jnp.bfloat16)
        back_slots = jnp.dot(
            back_freq.T, sounding_table, preferred_element_type=jnp.float32
        ).astype(jnp.bfloat16)
        return jnp.sum(
            sens_slots.astype(jnp.float32) * back_slots.astype(jnp.float32)[:, :, None], axis=0
        )

    def send_back(outgoing, extra):
        outgoing = jnp.concatenate(
            [
                outgoing.reshape(owners, 1, capacity * block_cells),
                extra.reshape(owners, 1, block_cells),
            ],
            axis=2,
        )
        outgoing = jnp.concatenate([outgoing] * members, axis=0)
        returned = lax.all_to_all(outgoing, ("grp", "snd"), 0, 0, tiled=True)
        returned = returned.reshape(members, owners, capacity + 1, block_cells)
        return returned[:, :, :capacity, :], returned[0, :, capacity, :]

    def first_contributions(weighted):
        back_freq = jnp.dot(
            weighted, gate_map.T, precision=precise, preferred_element_type=jnp.float32
        ).astype(jnp.bfloat16)
        contribution = jnp.einsum(
            "skfc,sf->skc", sensitivity, back_freq, preferred_element_type=jnp.float32
        )
        parts = jnp.einsum(
            "oqsk,xskc->xoqc",
            slot_hit.astype(jnp.bfloat16),
            split3(contribution),
            preferred_element_type=jnp.float32,
        )
        return ((parts[0] + parts[1]) + parts[2]).reshape(slots, block_cells)

    right_partial, first_extra = send_back(
        first_contributions(data_weight * data_resid),
        jnp.pad(
            request[:, None, :].astype(jnp.float32),
            ((0, 0), (0, 0), (0, block_cells - capacity)),
        ),
    )
    incoming = first_extra[:, :capacity].astype(jnp.int32)
    live_slot = incoming >= 0
    safe_index = jnp.maximum(incoming, 0)
    owner_table = jnp.logical_and(
        safe_index[None] == jnp.arange(blocks_dev, dtype=jnp.int32)[:, None, None],
        live_slot[None],
    )
    owner_table = jnp.broadcast_to(
        owner_table[:, None], (blocks_dev, members, owners, capacity)
    ).astype(jnp.bfloat16)
    reply_table = jnp.logical_and(
        safe_index[:, :, None] == jnp.arange(blocks_dev, dtype=jnp.int32)[None, None, :],
        live_slot[:, :, None],
    ).astype(jnp.bfloat16)

    def gather_cells(rows):
        parts = jnp.einsum(
            "rjoq,sjoqc->src", owner_table, split3(rows), preferred_element_type=jnp.float32
        )
        return (parts[0] + parts[1]) + parts[2]

    def pick_rows(field):
        parts = jnp.einsum(
            "oqr,src->soqc", reply_table, split3(field), preferred_element_type=jnp.float32
        )
        return (parts[0] + parts[1]) + parts[2]

    right_side = gather_cells(right_partial)
    model_step = jnp.zeros(reg_weight.shape, jnp.float32)
    residual = right_side
    direction = right_side
    fetched_dir = None
    norm_now = None
    for iteration in range(ITERS):
        local_norm = lane_total(residual * residual)
        replies = pick_rows(residual)
        replies = jnp.concatenate(
            [
                replies.reshape(owners, 1, capacity * block_cells),
                extra_row(local_norm).reshape(owners, 1, block_cells),
            ],
            axis=2,
        )
        arrived = lax.all_to_all(replies, "snd", 0, 0, tiled=True)
        arrived = arrived.reshape(owners, capacity + 1, block_cells)
        norm_next = jnp.sum(arrived[:, capacity, :], axis=0)
        fetched_res = arrived[:, :capacity].reshape(slots, block_cells)
        if iteration == 0:
            fetched_dir = fetched_res
        else:
            ratio = norm_next / norm_now
            direction = residual + ratio * direction
            fetched_dir = fetched_res + ratio * fetched_dir
        norm_now = norm_next
        forward_fetched = sounding_table[:, :, None] * fetched_dir.astype(jnp.bfloat16)[None]
        response = jnp.einsum(
            "spc,fpc->sf", forward_fetched, sens_slots, preferred_element_type=jnp.float32
        )
        partial_gates = jnp.dot(
            response, gate_map, precision=precise, preferred_element_type=jnp.float32
        )
        reg_curve = lane_total(reg_weight * direction * direction)
        predicted = lax.psum(partial_gates, "grp")
        weighted = data_weight * predicted
        local_curve = lane_total(predicted * weighted) + reg_curve
        image_partial, curve_extra = send_back(contributions(weighted), extra_row(local_curve))
        curvature = jnp.sum(curve_extra, axis=0)
        image_cells = gather_cells(image_partial) + reg_weight * direction
        step_size = norm_now / curvature
        model_step = model_step + step_size * direction
        residual = residual - step_size * image_cells
    return (model_step, residual)


def solution(mesh):
    in_specs = (
        P("snd", None, "grp", None),
        P("grp", None),
        P("snd", None),
        P("snd", None),
        P("snd", None),
        P("snd", None),
        P(),
    )
    out_specs = (P("snd", None), P("snd", None))
    return jax.shard_map(body, mesh=mesh, in_specs=in_specs, out_specs=out_specs, check_vma=False)
```
